32 devices in a mesh: grp: 2 (over y), gx: 4 (over z), gy: 2 (over x), col: 2 (over core).
Axes of the slice: x: 2, y: 2, z: 4, core: 2. Of those that a mesh axis runs over, the one named last changes fastest.
Arguments:
- x_act: bfloat16 [32, 32, 32, 128], P(('grp', 'gx'), 'gy'), parts along dimension 0, may hold values from -6 to 6
- grad_out: bfloat16 [32, 32, 32, 128], P(('grp', 'gx'), 'gy'), parts along dimension 0, may hold values from -6 to 6
- weight: bfloat16 [27, 128, 128], replicated, may hold values from -0.109375 to 0.109375
Outputs:
- grad_in: bfloat16 [32, 32, 32, 128], P(('grp', 'gx'), 'gy'), parts along dimension 0
- grad_weight: float32 [6912, 128], P(('grp', 'gx', 'gy'), 'col'), parts along dimension 0
The draws below stay inside these ranges and needn't reach their ends.
There are 2 independent parts, one for each index of `grp`. The reference program is written for one: setup_inputs(seed, part) draws one part's arguments, and reference() takes and returns one part's arrays. A program takes and returns all parts, laid end to end along the dimension named above; an argument that names none is the same for every part. Nothing has to cross between parts.
All inputs are finite; a program needn't handle non-finite values.
Results may differ from the reference program's by a relative error of at most 0.001.
Values may be sent and summed in bfloat16 or wider, within the bound.
No kernel may reach another device: no remote copies, remote signals or barrier semaphores. Data moves between devices by JAX's collectives and lax.ppermute only.
A program may use at most 64 MiB of HBM per device.

```python
import jax
import jax.numpy as jnp
from jax import lax

C = 128
DEPTH = 32
NX = 16
NY = 32


def raised(values, own_key, source, target, parts, factor):
    owner, partner = [(jnp.arange(values.shape[axis_at]) // (values.shape[axis_at] // parts)).reshape([-1 if axis == axis_at else 1 for axis in range(values.ndim)]) for axis_at in (source, target)]
    chosen = jax.random.permutation(own_key, parts)[partner]
    strong = (owner == chosen) | (owner == (partner + parts // 2) % parts)
    return jnp.where(strong, factor * values, values)


def levels(stream_key, dims, cuts, low, largest):
    loudness = 1.0
    for axis_at, blocks in cuts:
        draws = jax.random.uniform(jax.random.fold_in(jax.random.fold_in(stream_key, 6), axis_at), (blocks,), jnp.float32, low / len(cuts), largest / len(cuts))
        loudness = loudness * jnp.repeat(jnp.exp(draws), dims[axis_at] // blocks).reshape((-1,) + (1,) * (len(dims) - 1 - axis_at))
    return loudness


def scatter_about(rng, extent, deviation, bound, shards=(), held_as=jnp.bfloat16):
    entries = jax.random.normal(rng, extent, jnp.float32) * deviation
    if len(shards) > 0:
        entries = levels(rng, extent, shards, -0.22, 0.18) * entries
    return jnp.clip(entries, min=-bound, max=bound).astype(held_as)


def gaussian_with(rng, shape, spread, limit, cuts, heavy, held_as=jnp.bfloat16):
    result = spread * jax.random.normal(rng, shape, jnp.float32)
    if cuts:
        result = result * levels(rng, shape, cuts, -0.22, 0.18)
    return jnp.clip(raised(result, jax.random.fold_in(rng, 3), *heavy), -limit, limit).astype(held_as)


def setup_inputs(seed: int = 0, part: int = 0) -> dict:
    key_list = jax.random.split(jax.random.key(seed), 4)
    own_keys = jax.random.split(jax.random.fold_in(key_list[3], part), 4)
    x_act = gaussian_with(own_keys[0], (NX, NY, DEPTH, C), 1.0, 6.0, ((0, 4), (1, 2)), (0, 3, 4, 2.0))
    grad_out = scatter_about(own_keys[1], (NX, NY, DEPTH, C), 1.0, 6.0, ((0, 4), (1, 2)))
    weight = scatter_about(key_list[2], (27, C, C), (27 * C) ** -0.5, 0.109375)
    return dict(x_act=x_act, grad_out=grad_out, weight=weight)


def reference(x_act, grad_out, weight):
    hi = lax.Precision.HIGHEST
    xf = x_act.astype(jnp.float32)
    gf = grad_out.astype(jnp.float32)
    wf = weight.astype(jnp.float32)
    xpad = jnp.pad(xf, ((1, 1), (1, 1), (1, 1), (0, 0)))
    gpad = jnp.pad(gf, ((1, 1), (1, 1), (1, 1), (0, 0)))
    cells = NX * NY * DEPTH
    gflat = gf.reshape(cells, C)
    accum = jnp.zeros((cells, C), jnp.float32)
    pieces = []
    for a in range(3):
        for b in range(3):
            for c in range(3):
                tap = a * 9 + b * 3 + c
                gsl = gpad[2 - a:2 - a + NX, 2 - b:2 - b + NY, 2 - c:2 - c + DEPTH].reshape(cells, C)
                accum = accum + jnp.dot(gsl, wf[tap].T, precision=hi)
                xsl = xpad[a:a + NX, b:b + NY, c:c + DEPTH].reshape(cells, C)
                pieces.append(jnp.dot(xsl.T, gflat, precision=hi))
    grad_in = accum.reshape(NX, NY, DEPTH, C).astype(jnp.bfloat16)
    weight_sum = jnp.concatenate(pieces, axis=0)
    grad_weight = weight_sum / jnp.sqrt(jnp.float32(cells))
    return (grad_in, grad_weight)
```

```python
import jax
import jax.numpy as jnp
from jax import lax
from jax.sharding import PartitionSpec as P


def with_halo(cells, sides, width):
    for axis, dim in sides:
        count = lax.axis_size(axis)
        ends = count - 1
        head = lax.slice_in_dim(cells, 0, width, axis=dim)
        tail = lax.slice_in_dim(cells, cells.shape[dim] - width, cells.shape[dim], axis=dim)
        cells = jnp.concatenate(
            [
                lax.ppermute(tail, axis, [(i, (i + 1) % count) for i in range(ends)]),
                cells,
                lax.ppermute(head, axis, [((i + 1) % count, i) for i in range(ends)]),
            ],
            axis=dim,
        )
    return cells


def depth_taps(block, starts, depth):
    return jnp.concatenate([lax.slice_in_dim(block, s, s + depth, axis=2) for s in starts], axis=3)


def kernel_rows(weight, a, b):
    first = a * 9 + b * 3
    three = weight[first : first + 3]
    return jnp.transpose(three, (0, 2, 1)).reshape(3 * weight.shape[2], weight.shape[1])


def local_terms(gslab, x_rows, weight_part, size_x, size_y, depth):
    chans = x_rows.shape[3]
    width = weight_part.shape[2]
    cells = size_x * size_y * depth
    xflat = x_rows.reshape(cells, chans)
    contract_rows = (((0,), (0,)), ((), ()))
    accum = jnp.zeros((cells, chans), jnp.float32)
    pieces = []
    for a in range(3):
        for b in range(3):
            block = gslab[2 - a : 2 - a + size_x, 2 - b : 2 - b + size_y]
            stacked = depth_taps(block, (2, 1, 0), depth).reshape(cells, 3 * width)
            accum = accum + jnp.dot(
                stacked, kernel_rows(weight_part, a, b), preferred_element_type=jnp.float32
            )
            term = lax.dot_general(
                xflat, stacked, contract_rows, preferred_element_type=jnp.float32
            )
            pieces.append(
                jnp.transpose(term.reshape(chans, 3, width), (1, 0, 2)).reshape(3 * chans, width)
            )
    return (accum.reshape(size_x, size_y, depth, chans), jnp.concatenate(pieces, axis=0))


def scatter_sum(blocks, axis, dim):
    count = lax.axis_size(axis)
    if count == 1:
        return lax.index_in_dim(blocks, 0, dim, keepdims=False)
    if count > 4:
        return lax.psum_scatter(blocks, axis, scatter_dimension=dim, tiled=False)
    me = lax.axis_index(axis)
    total = lax.dynamic_index_in_dim(blocks, me, dim, keepdims=False)
    for shift in range(1, count):
        for sign in (1, -1):
            step = sign * shift
            pairs = [(j, j + step) for j in range(count) if 0 <= j + step < count]
            target = jnp.clip(me + step, 0, count - 1)
            part = lax.dynamic_index_in_dim(blocks, target, dim, keepdims=False)
            total = total + lax.ppermute(part, axis, pairs)
    return total


def on_device(x_act, grad_out, weight):
    size_x, size_y, depth, chans = x_act.shape
    ncores = lax.axis_size("col")
    half = chans // ncores
    offset = lax.axis_index("col") * half
    grad_share = lax.dynamic_slice_in_dim(grad_out, offset, half, 3)
    weight_share = lax.dynamic_slice_in_dim(weight, offset, half, 2)
    grim = with_halo(grad_share, (("gx", 0), ("gy", 1)), 1)
    gdeep = jnp.pad(grim, ((0, 0), (0, 0), (1, 1), (0, 0)))
    inner, weight_terms = local_terms(gdeep, x_act, weight_share, size_x, size_y, depth)
    grad_in = lax.psum(inner, "col").astype(jnp.bfloat16)
    nx = lax.axis_size("gx")
    ny = lax.axis_size("gy")
    blocks = weight_terms.reshape(nx, ny, weight_terms.shape[0] // (nx * ny), weight_terms.shape[1])
    owned = scatter_sum(scatter_sum(blocks, "gy", 1), "gx", 0)
    total_cells = size_x * lax.axis_size("gx") * size_y * lax.axis_size("gy") * depth
    grad_weight = owned / jnp.sqrt(jnp.float32(total_cells))
    return (grad_in, grad_weight)


def solution(mesh):
    return jax.shard_map(
        on_device,
        mesh=mesh,
        in_specs=(P(("grp", "gx"), "gy", None, None), P(("grp", "gx"), "gy", None, None), P()),
        out_specs=(P(("grp", "gx"), "gy", None, None), P(("grp", "gx", "gy"), "col")),
        check_vma=False,
    )
```

```python
import jax
import jax.numpy as jnp
from jax import lax
from jax.sharding import PartitionSpec as P


def with_halo(cells, sides, width):
    for axis, dim in sides:
        count = lax.axis_size(axis)
        ends = count - 1
        head = lax.slice_in_dim(cells, 0, width, axis=dim)
        tail = lax.slice_in_dim(cells, cells.shape[dim] - width, cells.shape[dim], axis=dim)
        cells = jnp.concatenate(
            [
                lax.ppermute(tail, axis, [(i, (i + 1) % count) for i in range(ends)]),
                cells,
                lax.ppermute(head, axis, [((i + 1) % count, i) for i in range(ends)]),
            ],
            axis=dim,
        )
    return cells


def scatter_sum(blocks, axis, dim):
    count = lax.axis_size(axis)
    if count == 1:
        return lax.index_in_dim(blocks, 0, dim, keepdims=False)
    if count > 4:
        return lax.psum_scatter(blocks, axis, scatter_dimension=dim, tiled=False)
    me = lax.axis_index(axis)
    total = lax.dynamic_index_in_dim(blocks, me, dim, keepdims=False)
    for shift in range(1, count):
        up = [(j, j + shift) for j in range(count) if j + shift < count]
        down = [(j, j - shift) for j in range(count) if j - shift >= 0]
        if {s for s, _ in up} & {s for s, _ in down}:
            groups = [(up, me + shift), (down, me - shift)]
        else:
            groups = [(up + down, jnp.where(me + shift < count, me + shift, me - shift))]
        for pairs, target in groups:
            part = lax.dynamic_index_in_dim(blocks, jnp.clip(target, 0, count - 1), dim, keepdims=False)
            total = total + lax.ppermute(part, axis, pairs)
    return total


def on_device(x_act, grad_out, weight):
    size_x, size_y, depth, chans = x_act.shape
    ncores = lax.axis_size("col")
    half = weight.shape[2] // ncores
    offset = lax.axis_index("col") * half
    gh = with_halo(grad_out, (("gx", 0), ("gy", 1)), 1)
    taps = weight.reshape(3, 3, 3, chans, weight.shape[2])
    kflip = jnp.transpose(taps[::-1, ::-1, ::-1], (0, 1, 2, 4, 3))
    pad = [(0, 0), (0, 0), (1, 1)]
    inner = lax.conv_general_dilated(
        gh[None], kflip, (1, 1, 1), pad,
        dimension_numbers=("NDHWC", "DHWIO", "NDHWC"),
        preferred_element_type=jnp.float32,
    )[0]
    grad_in = inner.astype(jnp.bfloat16)
    gshare = lax.dynamic_slice_in_dim(gh, offset, half, 3)
    filter_dims = lax.ConvDimensionNumbers(
        lhs_spec=(4, 0, 1, 2, 3), rhs_spec=(4, 0, 1, 2, 3), out_spec=(3, 4, 0, 1, 2)
    )
    kgrad = lax.conv_general_dilated(
        gshare[None], x_act[None], (1, 1, 1), pad,
        dimension_numbers=filter_dims,
        preferred_element_type=jnp.float32,
    )
    weight_terms = jnp.transpose(kgrad[::-1, ::-1, ::-1], (0, 1, 2, 4, 3)).reshape(27 * chans, half)
    nx = lax.axis_size("gx")
    ny = lax.axis_size("gy")
    blocks = weight_terms.reshape(nx, ny, weight_terms.shape[0] // (nx * ny), half)
    owned = scatter_sum(scatter_sum(blocks, "gy", 1), "gx", 0)
    total_cells = size_x * lax.axis_size("gx") * size_y * lax.axis_size("gy") * depth
    grad_weight = owned / jnp.sqrt(jnp.float32(total_cells))
    return (grad_in, grad_weight)


def solution(mesh):
    return jax.shard_map(
        on_device,
        mesh=mesh,
        in_specs=(P(("grp", "gx"), "gy", None, None), P(("grp", "gx"), "gy", None, None), P()),
        out_specs=(P(("grp", "gx"), "gy", None, None), P(("grp", "gx", "gy"), "col")),
        check_vma=False,
    )
```

```python
import jax
import jax.numpy as jnp
from jax import lax
from jax.sharding import PartitionSpec as P


def with_halo(cells, sides, width):
    for axis, dim in sides:
        count = lax.axis_size(axis)
        head = lax.slice_in_dim(cells, 0, width, axis=dim)
        tail = lax.slice_in_dim(cells, cells.shape[dim] - width, cells.shape[dim], axis=dim)
        if count == 1:
            low = jnp.zeros_like(tail)
            high = jnp.zeros_like(head)
        elif count == 2:
            me = lax.axis_index(axis)
            got = lax.ppermute(jnp.where(me == 0, tail, head), axis, [(0, 1), (1, 0)])
            low = jnp.where(me == 1, got, jnp.zeros_like(got))
            high = jnp.where(me == 0, got, jnp.zeros_like(got))
        else:
            low = lax.ppermute(tail, axis, [(i, i + 1) for i in range(count - 1)])
            high = lax.ppermute(head, axis, [(i + 1, i) for i in range(count - 1)])
        cells = jnp.concatenate([low, cells, high], axis=dim)
    return cells


def scatter_sum(blocks, axis, dim):
    count = lax.axis_size(axis)
    if count == 1:
        return lax.index_in_dim(blocks, 0, dim, keepdims=False)
    if count > 4:
        return lax.psum_scatter(blocks, axis, scatter_dimension=dim, tiled=False)
    me = lax.axis_index(axis)
    total = lax.dynamic_index_in_dim(blocks, me, dim, keepdims=False)
    for shift in range(1, count):
        up = [(j, j + shift) for j in range(count) if j + shift < count]
        down = [(j, j - shift) for j in range(count) if j - shift >= 0]
        if {s for s, _ in up} & {s for s, _ in down}:
            groups = [(up, me + shift), (down, me - shift)]
        else:
            groups = [(up + down, jnp.where(me + shift < count, me + shift, me - shift))]
        for pairs, target in groups:
            part = lax.dynamic_index_in_dim(blocks, jnp.clip(target, 0, count - 1), dim, keepdims=False)
            total = total + lax.ppermute(part, axis, pairs)
    return total


def on_device(x_act, grad_out, weight):
    size_x, size_y, depth, chans = x_act.shape
    ncores = lax.axis_size("col")
    half = weight.shape[2] // ncores
    offset = lax.axis_index("col") * half
    gh = with_halo(grad_out, (("gy", 1), ("gx", 0)), 1)
    taps = weight.reshape(3, 3, 3, chans, weight.shape[2])
    kflip = jnp.transpose(taps[::-1, ::-1, ::-1], (0, 1, 2, 4, 3))
    pad = [(0, 0), (0, 0), (1, 1)]
    inner = lax.conv_general_dilated(
        gh[None], kflip, (1, 1, 1), pad,
        dimension_numbers=("NDHWC", "DHWIO", "NDHWC"),
        preferred_element_type=jnp.float32,
    )[0]
    grad_in = inner.astype(jnp.bfloat16)
    gshare = lax.dynamic_slice_in_dim(gh, offset, half, 3)
    gdeep = jnp.pad(gshare, ((0, 0), (0, 0), (1, 1), (0, 0)))
    stack = jnp.concatenate([lax.slice_in_dim(gdeep, 2 - c, 2 - c + depth, axis=2) for c in range(3)], axis=3)
    pieces = []
    for a in range(3):
        for b in range(3):
            window = stack[2 - a : 2 - a + size_x, 2 - b : 2 - b + size_y]
            term = lax.dot_general(
                x_act, window, (((0, 1, 2), (0, 1, 2)), ((), ())), preferred_element_type=jnp.float32
            )
            pieces.append(jnp.transpose(term.reshape(chans, 3, half), (1, 0, 2)).reshape(3 * chans, half))
    weight_terms = jnp.concatenate(pieces, axis=0)
    nx = lax.axis_size("gx")
    ny = lax.axis_size("gy")
    blocks = weight_terms.reshape(nx, ny, weight_terms.shape[0] // (nx * ny), half)
    owned = scatter_sum(scatter_sum(blocks, "gy", 1), "gx", 0)
    total_cells = size_x * lax.axis_size("gx") * size_y * lax.axis_size("gy") * depth
    grad_weight = owned / jnp.sqrt(jnp.float32(total_cells))
    return (grad_in, grad_weight)


def solution(mesh):
    return jax.shard_map(
        on_device,
        mesh=mesh,
        in_specs=(P(("grp", "gx"), "gy", None, None), P(("grp", "gx"), "gy", None, None), P()),
        out_specs=(P(("grp", "gx"), "gy", None, None), P(("grp", "gx", "gy"), "col")),
        check_vma=False,
    )
```

```python
import jax
import jax.numpy as jnp
from jax import lax
from jax.sharding import PartitionSpec as P


def with_halo(cells, sides, width):
    for axis, dim in sides:
        count = lax.axis_size(axis)
        head = lax.slice_in_dim(cells, 0, width, axis=dim)
        tail = lax.slice_in_dim(cells, cells.shape[dim] - width, cells.shape[dim], axis=dim)
        if count == 1:
            low = jnp.zeros_like(tail)
            high = jnp.zeros_like(head)
        elif count == 2:
            me = lax.axis_index(axis)
            got = lax.ppermute(jnp.where(me == 0, tail, head), axis, [(0, 1), (1, 0)])
            low = jnp.where(me == 1, got, jnp.zeros_like(got))
            high = jnp.where(me == 0, got, jnp.zeros_like(got))
        else:
            low = lax.ppermute(tail, axis, [(i, i + 1) for i in range(count - 1)])
            high = lax.ppermute(head, axis, [(i + 1, i) for i in range(count - 1)])
        cells = jnp.concatenate([low, cells, high], axis=dim)
    return cells


def scatter_sum(blocks, axis, dim):
    count = lax.axis_size(axis)
    if count == 1:
        return lax.index_in_dim(blocks, 0, dim, keepdims=False)
    if count > 4:
        return lax.psum_scatter(blocks, axis, scatter_dimension=dim, tiled=False)
    me = lax.axis_index(axis)
    total = lax.dynamic_index_in_dim(blocks, me, dim, keepdims=False)
    for shift in range(1, count):
        part = lax.dynamic_index_in_dim(blocks, (me + shift) % count, dim, keepdims=False)
        total = total + lax.ppermute(part, axis, [(j, (j + shift) % count) for j in range(count)])
    return total


def on_device(x_act, grad_out, weight):
    size_x, size_y, depth, chans = x_act.shape
    ncores = lax.axis_size("col")
    half = weight.shape[2] // ncores
    offset = lax.axis_index("col") * half
    gh = with_halo(grad_out, (("gy", 1), ("gx", 0)), 1)
    taps = weight.reshape(3, 3, 3, chans, weight.shape[2])
    kflip = jnp.transpose(taps[::-1, ::-1, ::-1], (0, 1, 2, 4, 3))
    pad = [(0, 0), (0, 0), (1, 1)]
    inner = lax.conv_general_dilated(
        gh[None], kflip, (1, 1, 1), pad,
        dimension_numbers=("NDHWC", "DHWIO", "NDHWC"),
        preferred_element_type=jnp.float32,
    )[0]
    grad_in = inner.astype(jnp.bfloat16)
    gshare = lax.dynamic_slice_in_dim(gh, offset, half, 3)
    gdeep = jnp.pad(gshare, ((0, 0), (0, 0), (1, 1), (0, 0)))
    stack = jnp.concatenate([lax.slice_in_dim(gdeep, 2 - c, 2 - c + depth, axis=2) for c in range(3)], axis=3)
    pieces = []
    for a in range(3):
        for b in range(3):
            window = stack[2 - a : 2 - a + size_x, 2 - b : 2 - b + size_y]
            term = lax.dot_general(
                x_act, window, (((0, 1, 2), (0, 1, 2)), ((), ())), preferred_element_type=jnp.float32
            )
            pieces.append(jnp.transpose(term.reshape(chans, 3, half), (1, 0, 2)).reshape(3 * chans, half))
    weight_terms = jnp.concatenate(pieces, axis=0)
    nx = lax.axis_size("gx")
    ny = lax.axis_size("gy")
    blocks = weight_terms.reshape(nx, ny, weight_terms.shape[0] // (nx * ny), half)
    owned = scatter_sum(scatter_sum(blocks, "gy", 1), "gx", 0)
    total_cells = size_x * lax.axis_size("gx") * size_y * lax.axis_size("gy") * depth
    grad_weight = owned / jnp.sqrt(jnp.float32(total_cells))
    return (grad_in, grad_weight)


def solution(mesh):
    return jax.shard_map(
        on_device,
        mesh=mesh,
        in_specs=(P(("grp", "gx"), "gy", None, None), P(("grp", "gx"), "gy", None, None), P()),
        out_specs=(P(("grp", "gx"), "gy", None, None), P(("grp", "gx", "gy"), "col")),
        check_vma=False,
    )
```

```python
import jax
import jax.numpy as jnp
from jax import lax
from jax.sharding import PartitionSpec as P


def with_halo(cells, sides, width):
    for axis, dim in sides:
        count = lax.axis_size(axis)
        head = lax.slice_in_dim(cells, 0, width, axis=dim)
        tail = lax.slice_in_dim(cells, cells.shape[dim] - width, cells.shape[dim], axis=dim)
        if count == 1:
            low = jnp.zeros_like(tail)
            high = jnp.zeros_like(head)
        elif count == 2:
            me = lax.axis_index(axis)
            got = lax.ppermute(jnp.where(me == 0, tail, head), axis, [(0, 1), (1, 0)])
            low = jnp.where(me == 1, got, jnp.zeros_like(got))
            high = jnp.where(me == 0, got, jnp.zeros_like(got))
        else:
            low = lax.ppermute(tail, axis, [(i, i + 1) for i in range(count - 1)])
            high = lax.ppermute(head, axis, [(i + 1, i) for i in range(count - 1)])
        cells = jnp.concatenate([low, cells, high], axis=dim)
    return cells


def edge_pair(head, tail, axis):
    count = lax.axis_size(axis)
    if count == 1:
        return jnp.zeros_like(tail), jnp.zeros_like(head)
    if count == 2:
        me = lax.axis_index(axis)
        got = lax.ppermute(jnp.where(me == 0, tail, head), axis, [(0, 1), (1, 0)])
        return jnp.where(me == 1, got, jnp.zeros_like(got)), jnp.where(me == 0, got, jnp.zeros_like(got))
    low = lax.ppermute(tail, axis, [(i, i + 1) for i in range(count - 1)])
    high = lax.ppermute(head, axis, [(i + 1, i) for i in range(count - 1)])
    return low, high


def with_halo_one_stage(cells):
    nx = lax.axis_size("gx")
    ix = lax.axis_index("gx")
    iy = lax.axis_index("gy")
    low_r, high_r = edge_pair(cells[:1], cells[-1:], "gx")
    low_c, high_c = edge_pair(cells[:, :1], cells[:, -1:], "gy")
    both = ("gx", "gy")
    zero = jnp.zeros_like(cells[:1, :1])
    if nx > 1:
        ahead = [(x * 2 + y, (x + 1) * 2 + 1 - y) for x in range(nx - 1) for y in range(2)]
        behind = [((x + 1) * 2 + y, x * 2 + 1 - y) for x in range(nx - 1) for y in range(2)]
        from_low = lax.ppermute(jnp.where(iy == 0, cells[-1:, -1:], cells[-1:, :1]), both, ahead)
        from_high = lax.ppermute(jnp.where(iy == 0, cells[:1, -1:], cells[:1, :1]), both, behind)
    else:
        from_low = from_high = zero
    top = jnp.concatenate(
        [jnp.where(iy == 1, from_low, zero), low_r, jnp.where(iy == 0, from_low, zero)], axis=1
    )
    bottom = jnp.concatenate(
        [jnp.where(iy == 1, from_high, zero), high_r, jnp.where(iy == 0, from_high, zero)], axis=1
    )
    middle = jnp.concatenate([low_c, cells, high_c], axis=1)
    return jnp.concatenate([top, middle, bottom], axis=0)


def scatter_sum(blocks, axis, dim):
    count = lax.axis_size(axis)
    if count == 1:
        return lax.index_in_dim(blocks, 0, dim, keepdims=False)
    if count > 4:
        return lax.psum_scatter(blocks, axis, scatter_dimension=dim, tiled=False)
    me = lax.axis_index(axis)
    total = lax.dynamic_index_in_dim(blocks, me, dim, keepdims=False)
    for shift in range(1, count):
        part = lax.dynamic_index_in_dim(blocks, (me + shift) % count, dim, keepdims=False)
        total = total + lax.ppermute(part, axis, [(j, (j + shift) % count) for j in range(count)])
    return total


def on_device(x_act, grad_out, weight):
    size_x, size_y, depth, chans = x_act.shape
    ncores = lax.axis_size("col")
    half = weight.shape[2] // ncores
    offset = lax.axis_index("col") * half
    if lax.axis_size("gy") == 2:
        gh = with_halo_one_stage(grad_out)
    else:
        gh = with_halo(grad_out, (("gy", 1), ("gx", 0)), 1)
    taps = weight.reshape(3, 3, 3, chans, weight.shape[2])
    kflip = jnp.transpose(taps[::-1, ::-1, ::-1], (0, 1, 2, 4, 3))
    pad = [(0, 0), (0, 0), (1, 1)]
    inner = lax.conv_general_dilated(
        gh[None], kflip, (1, 1, 1), pad,
        dimension_numbers=("NDHWC", "DHWIO", "NDHWC"),
        preferred_element_type=jnp.float32,
    )[0]
    grad_in = inner.astype(jnp.bfloat16)
    gshare = lax.dynamic_slice_in_dim(gh, offset, half, 3)
    gdeep = jnp.pad(gshare, ((0, 0), (0, 0), (1, 1), (0, 0)))
    stack = jnp.concatenate([lax.slice_in_dim(gdeep, 2 - c, 2 - c + depth, axis=2) for c in range(3)], axis=3)
    pieces = []
    for a in range(3):
        for b in range(3):
            window = stack[2 - a : 2 - a + size_x, 2 - b : 2 - b + size_y]
            term = lax.dot_general(
                x_act, window, (((0, 1, 2), (0, 1, 2)), ((), ())), preferred_element_type=jnp.float32
            )
            pieces.append(jnp.transpose(term.reshape(chans, 3, half), (1, 0, 2)).reshape(3 * chans, half))
    weight_terms = jnp.concatenate(pieces, axis=0)
    nx = lax.axis_size("gx")
    ny = lax.axis_size("gy")
    blocks = weight_terms.reshape(nx, ny, weight_terms.shape[0] // (nx * ny), half)
    owned = scatter_sum(scatter_sum(blocks, "gy", 1), "gx", 0)
    total_cells = size_x * lax.axis_size("gx") * size_y * lax.axis_size("gy") * depth
    grad_weight = owned / jnp.sqrt(jnp.float32(total_cells))
    return (grad_in, grad_weight)


def solution(mesh):
    return jax.shard_map(
        on_device,
        mesh=mesh,
        in_specs=(P(("grp", "gx"), "gy", None, None), P(("grp", "gx"), "gy", None, None), P()),
        out_specs=(P(("grp", "gx"), "gy", None, None), P(("grp", "gx", "gy"), "col")),
        check_vma=False,
    )
```

```python
import jax
import jax.numpy as jnp
from jax import lax
from jax.sharding import PartitionSpec as P


def halo_pieces(cells, sides, width):
    got = []
    for axis, dim in sides:
        count = lax.axis_size(axis)
        head = lax.slice_in_dim(cells, 0, width, axis=dim)
        tail = lax.slice_in_dim(cells, cells.shape[dim] - width, cells.shape[dim], axis=dim)
        if count == 1:
            low = jnp.zeros_like(tail)
            high = jnp.zeros_like(head)
        elif count == 2:
            me = lax.axis_index(axis)
            recv = lax.ppermute(jnp.where(me == 0, tail, head), axis, [(0, 1), (1, 0)])
            low = jnp.where(me == 1, recv, jnp.zeros_like(recv))
            high = jnp.where(me == 0, recv, jnp.zeros_like(recv))
        else:
            low = lax.ppermute(tail, axis, [(i, i + 1) for i in range(count - 1)])
            high = lax.ppermute(head, axis, [(i + 1, i) for i in range(count - 1)])
        got.append((dim, low, high))
        cells = jnp.concatenate([low, cells, high], axis=dim)
    return got


def assemble(cells, got, channels):
    cells = lax.slice_in_dim(cells, channels[0], channels[1], axis=3)
    for dim, low, high in got:
        cells = jnp.concatenate(
            [lax.slice_in_dim(low, channels[0], channels[1], axis=3), cells,
             lax.slice_in_dim(high, channels[0], channels[1], axis=3)],
            axis=dim,
        )
    return cells


def scatter_sum(blocks, axis, dim):
    count = lax.axis_size(axis)
    if count == 1:
        return lax.index_in_dim(blocks, 0, dim, keepdims=False)
    if count > 4:
        return lax.psum_scatter(blocks, axis, scatter_dimension=dim, tiled=False)
    me = lax.axis_index(axis)
    total = lax.dynamic_index_in_dim(blocks, me, dim, keepdims=False)
    for shift in range(1, count):
        part = lax.dynamic_index_in_dim(blocks, (me + shift) % count, dim, keepdims=False)
        total = total + lax.ppermute(part, axis, [(j, (j + shift) % count) for j in range(count)])
    return total


def on_device(x_act, grad_out, weight):
    size_x, size_y, depth, chans = x_act.shape
    ncores = lax.axis_size("col")
    half = weight.shape[2] // ncores
    offset = lax.axis_index("col") * half
    got = halo_pieces(grad_out, (("gy", 1), ("gx", 0)), 1)
    gh = assemble(grad_out, got, (0, chans))
    taps = weight.reshape(3, 3, 3, chans, weight.shape[2])
    kflip = jnp.transpose(taps[::-1, ::-1, ::-1], (0, 1, 2, 4, 3))
    pad = [(0, 0), (0, 0), (1, 1)]
    inner = lax.conv_general_dilated(
        gh[None], kflip, (1, 1, 1), pad,
        dimension_numbers=("NDHWC", "DHWIO", "NDHWC"),
        preferred_element_type=jnp.float32,
    )[0]
    grad_in = inner.astype(jnp.bfloat16)
    if ncores == 1:
        gshare = assemble(grad_out, got, (0, half))
    else:
        gshare = jnp.where(
            lax.axis_index("col") == 0,
            assemble(grad_out, got, (0, half)),
            assemble(grad_out, got, (half, 2 * half)),
        )
    gdeep = jnp.pad(gshare, ((0, 0), (0, 0), (1, 1), (0, 0)))
    stack = jnp.concatenate([lax.slice_in_dim(gdeep, 2 - c, 2 - c + depth, axis=2) for c in range(3)], axis=3)
    pieces = []
    for a in range(3):
        for b in range(3):
            window = stack[2 - a : 2 - a + size_x, 2 - b : 2 - b + size_y]
            term = lax.dot_general(
                x_act, window, (((0, 1, 2), (0, 1, 2)), ((), ())), preferred_element_type=jnp.float32
            )
            pieces.append(jnp.transpose(term.reshape(chans, 3, half), (1, 0, 2)).reshape(3 * chans, half))
    weight_terms = jnp.concatenate(pieces, axis=0)
    nx = lax.axis_size("gx")
    ny = lax.axis_size("gy")
    blocks = weight_terms.reshape(nx, ny, weight_terms.shape[0] // (nx * ny), half)
    owned = scatter_sum(scatter_sum(blocks, "gy", 1), "gx", 0)
    total_cells = size_x * lax.axis_size("gx") * size_y * lax.axis_size("gy") * depth
    grad_weight = owned / jnp.sqrt(jnp.float32(total_cells))
    return (grad_in, grad_weight)


def solution(mesh):
    return jax.shard_map(
        on_device,
        mesh=mesh,
        in_specs=(P(("grp", "gx"), "gy", None, None), P(("grp", "gx"), "gy", None, None), P()),
        out_specs=(P(("grp", "gx"), "gy", None, None), P(("grp", "gx", "gy"), "col")),
        check_vma=False,
    )
```

```python
import jax
import jax.numpy as jnp
from jax import lax
from jax.experimental.layout import Layout, with_layout_constraint
from jax.sharding import PartitionSpec as P


def halo_pieces(cells, sides, width):
    got = []
    for axis, dim in sides:
        count = lax.axis_size(axis)
        head = lax.slice_in_dim(cells, 0, width, axis=dim)
        tail = lax.slice_in_dim(cells, cells.shape[dim] - width, cells.shape[dim], axis=dim)
        if count == 1:
            low = jnp.zeros_like(tail)
            high = jnp.zeros_like(head)
        elif count == 2:
            me = lax.axis_index(axis)
            recv = lax.ppermute(jnp.where(me == 0, tail, head), axis, [(0, 1), (1, 0)])
            low = jnp.where(me == 1, recv, jnp.zeros_like(recv))
            high = jnp.where(me == 0, recv, jnp.zeros_like(recv))
        else:
            low = lax.ppermute(tail, axis, [(i, i + 1) for i in range(count - 1)])
            high = lax.ppermute(head, axis, [(i + 1, i) for i in range(count - 1)])
        got.append((dim, low, high))
        cells = jnp.concatenate([low, cells, high], axis=dim)
    return got


def assemble(cells, got, channels):
    cells = lax.slice_in_dim(cells, channels[0], channels[1], axis=3)
    for dim, low, high in got:
        cells = jnp.concatenate(
            [lax.slice_in_dim(low, channels[0], channels[1], axis=3), cells,
             lax.slice_in_dim(high, channels[0], channels[1], axis=3)],
            axis=dim,
        )
    return cells


def scatter_sum(blocks, axis, dim):
    count = lax.axis_size(axis)
    if count == 1:
        return lax.index_in_dim(blocks, 0, dim, keepdims=False)
    if count > 4:
        return lax.psum_scatter(blocks, axis, scatter_dimension=dim, tiled=False)
    me = lax.axis_index(axis)
    total = lax.dynamic_index_in_dim(blocks, me, dim, keepdims=False)
    for shift in range(1, count):
        part = lax.dynamic_index_in_dim(blocks, (me + shift) % count, dim, keepdims=False)
        total = total + lax.ppermute(part, axis, [(j, (j + shift) % count) for j in range(count)])
    return total


def on_device(x_act, grad_out, weight):
    size_x, size_y, depth, chans = x_act.shape
    ncores = lax.axis_size("col")
    half = weight.shape[2] // ncores
    offset = lax.axis_index("col") * half
    got = halo_pieces(grad_out, (("gy", 1), ("gx", 0)), 1)
    gh = assemble(grad_out, got, (0, chans))
    taps = weight.reshape(3, 3, 3, chans, weight.shape[2])
    kflip = jnp.transpose(taps[::-1, ::-1, ::-1], (0, 1, 2, 4, 3))
    pad = [(0, 0), (0, 0), (1, 1)]
    inner = lax.conv_general_dilated(
        gh[None], kflip, (1, 1, 1), pad,
        dimension_numbers=("NDHWC", "DHWIO", "NDHWC"),
        preferred_element_type=jnp.float32,
    )[0]
    grad_in = inner.astype(jnp.bfloat16)
    if ncores == 1:
        gshare = assemble(grad_out, got, (0, half))
    else:
        gshare = jnp.where(
            lax.axis_index("col") == 0,
            assemble(grad_out, got, (0, half)),
            assemble(grad_out, got, (half, 2 * half)),
        )
    gdeep = jnp.pad(gshare, ((0, 0), (0, 0), (1, 1), (0, 0)))
    stack = jnp.concatenate([lax.slice_in_dim(gdeep, 2 - c, 2 - c + depth, axis=2) for c in range(3)], axis=3)
    pieces = []
    for a in range(3):
        for b in range(3):
            window = stack[2 - a : 2 - a + size_x, 2 - b : 2 - b + size_y]
            term = lax.dot_general(
                x_act, window, (((0, 1, 2), (0, 1, 2)), ((), ())), preferred_element_type=jnp.float32
            )
            pieces.append(jnp.transpose(term.reshape(chans, 3, half), (1, 0, 2)).reshape(3 * chans, half))
    weight_terms = with_layout_constraint(jnp.concatenate(pieces, axis=0), Layout(major_to_minor=(0, 1)))
    nx = lax.axis_size("gx")
    ny = lax.axis_size("gy")
    blocks = weight_terms.reshape(nx, ny, weight_terms.shape[0] // (nx * ny), half)
    rows_major = Layout(major_to_minor=(0, 1, 2, 3))
    blocks = with_layout_constraint(blocks, rows_major)
    partial = with_layout_constraint(scatter_sum(blocks, "gy", 1), Layout(major_to_minor=(0, 1, 2)))
    owned = with_layout_constraint(scatter_sum(partial, "gx", 0), Layout(major_to_minor=(0, 1)))
    total_cells = size_x * lax.axis_size("gx") * size_y * lax.axis_size("gy") * depth
    grad_weight = owned / jnp.sqrt(jnp.float32(total_cells))
    return (grad_in, grad_weight)


def solution(mesh):
    return jax.shard_map(
        on_device,
        mesh=mesh,
        in_specs=(P(("grp", "gx"), "gy", None, None), P(("grp", "gx"), "gy", None, None), P()),
        out_specs=(P(("grp", "gx"), "gy", None, None), P(("grp", "gx", "gy"), "col")),
        check_vma=False,
    )
```

```python
import jax
import jax.numpy as jnp
from jax import lax
from jax.sharding import PartitionSpec as P


def with_halo(cells, sides, width):
    for axis, dim in sides:
        count = lax.axis_size(axis)
        head = lax.slice_in_dim(cells, 0, width, axis=dim)
        tail = lax.slice_in_dim(cells, cells.shape[dim] - width, cells.shape[dim], axis=dim)
        if count == 1:
            low = jnp.zeros_like(tail)
            high = jnp.zeros_like(head)
        elif count == 2:
            me = lax.axis_index(axis)
            got = lax.ppermute(jnp.where(me == 0, tail, head), axis, [(0, 1), (1, 0)])
            low = jnp.where(me == 1, got, jnp.zeros_like(got))
            high = jnp.where(me == 0, got, jnp.zeros_like(got))
        else:
            me = lax.axis_index(axis)
            low = lax.ppermute(tail, axis, [(i, (i + 1) % count) for i in range(count)])
            high = lax.ppermute(head, axis, [((i + 1) % count, i) for i in range(count)])
            low = jnp.where(me == 0, jnp.zeros_like(low), low)
            high = jnp.where(me == count - 1, jnp.zeros_like(high), high)
        cells = jnp.concatenate([low, cells, high], axis=dim)
    return cells


def scatter_sum(blocks, axis, dim):
    count = lax.axis_size(axis)
    if count == 1:
        return lax.index_in_dim(blocks, 0, dim, keepdims=False)
    if count > 4:
        return lax.psum_scatter(blocks, axis, scatter_dimension=dim, tiled=False)
    me = lax.axis_index(axis)
    total = lax.dynamic_index_in_dim(blocks, me, dim, keepdims=False)
    for shift in range(1, count):
        part = lax.dynamic_index_in_dim(blocks, (me + shift) % count, dim, keepdims=False)
        total = total + lax.ppermute(part, axis, [(j, (j + shift) % count) for j in range(count)])
    return total


def on_device(x_act, grad_out, weight):
    size_x, size_y, depth, chans = x_act.shape
    ncores = lax.axis_size("col")
    half = weight.shape[2] // ncores
    offset = lax.axis_index("col") * half
    gh = with_halo(grad_out, (("gy", 1), ("gx", 0)), 1)
    taps = weight.reshape(3, 3, 3, chans, weight.shape[2])
    kflip = jnp.transpose(taps[::-1, ::-1, ::-1], (0, 1, 2, 4, 3))
    pad = [(0, 0), (0, 0), (1, 1)]
    inner = lax.conv_general_dilated(
        gh[None], kflip, (1, 1, 1), pad,
        dimension_numbers=("NDHWC", "DHWIO", "NDHWC"),
        preferred_element_type=jnp.float32,
    )[0]
    grad_in = inner.astype(jnp.bfloat16)
    gshare = lax.dynamic_slice_in_dim(gh, offset, half, 3)
    gdeep = jnp.pad(gshare, ((0, 0), (0, 0), (1, 1), (0, 0)))
    stack = jnp.concatenate([lax.slice_in_dim(gdeep, 2 - c, 2 - c + depth, axis=2) for c in range(3)], axis=3)
    pieces = []
    for a in range(3):
        for b in range(3):
            window = stack[2 - a : 2 - a + size_x, 2 - b : 2 - b + size_y]
            term = lax.dot_general(
                x_act, window, (((0, 1, 2), (0, 1, 2)), ((), ())), preferred_element_type=jnp.float32
            )
            pieces.append(jnp.transpose(term.reshape(chans, 3, half), (1, 0, 2)).reshape(3 * chans, half))
    weight_terms = jnp.concatenate(pieces, axis=0)
    nx = lax.axis_size("gx")
    ny = lax.axis_size("gy")
    blocks = weight_terms.reshape(nx, ny, weight_terms.shape[0] // (nx * ny), half)
    owned = scatter_sum(scatter_sum(blocks, "gy", 1), "gx", 0)
    total_cells = size_x * lax.axis_size("gx") * size_y * lax.axis_size("gy") * depth
    grad_weight = owned / jnp.sqrt(jnp.float32(total_cells))
    return (grad_in, grad_weight)


def solution(mesh):
    return jax.shard_map(
        on_device,
        mesh=mesh,
        in_specs=(P(("grp", "gx"), "gy", None, None), P(("grp", "gx"), "gy", None, None), P()),
        out_specs=(P(("grp", "gx"), "gy", None, None), P(("grp", "gx", "gy"), "col")),
        check_vma=False,
    )
```

```python
import jax
import jax.numpy as jnp
from jax import lax
from jax.sharding import PartitionSpec as P


def with_halo(cells, sides, width):
    for axis, dim in sides:
        count = lax.axis_size(axis)
        head = lax.slice_in_dim(cells, 0, width, axis=dim)
        tail = lax.slice_in_dim(cells, cells.shape[dim] - width, cells.shape[dim], axis=dim)
        if count == 1:
            low = jnp.zeros_like(tail)
            high = jnp.zeros_like(head)
        elif count == 2:
            me = lax.axis_index(axis)
            got = lax.ppermute(jnp.where(me == 0, tail, head), axis, [(0, 1), (1, 0)])
            low = jnp.where(me == 1, got, jnp.zeros_like(got))
            high = jnp.where(me == 0, got, jnp.zeros_like(got))
        else:
            low = lax.ppermute(tail, axis, [(i, i + 1) for i in range(count - 1)])
            high = lax.ppermute(head, axis, [(i + 1, i) for i in range(count - 1)])
        cells = jnp.concatenate([low, cells, high], axis=dim)
    return cells


def scatter_sum(blocks, axis, dim):
    count = lax.axis_size(axis)
    if count == 1:
        return lax.index_in_dim(blocks, 0, dim, keepdims=False)
    if count > 4:
        return lax.psum_scatter(blocks, axis, scatter_dimension=dim, tiled=False)
    me = lax.axis_index(axis)
    total = lax.dynamic_index_in_dim(blocks, me, dim, keepdims=False)
    for shift in range(1, count):
        part = lax.dynamic_index_in_dim(blocks, (me + shift) % count, dim, keepdims=False)
        total = total + lax.ppermute(part, axis, [(j, (j + shift) % count) for j in range(count)])
    return total


def on_device(x_act, grad_out, weight):
    size_x, size_y, depth, chans = x_act.shape
    ncores = lax.axis_size("col")
    half = weight.shape[2] // ncores
    offset = lax.axis_index("col") * half
    gh = with_halo(grad_out, (("gy", 1), ("gx", 0)), 1)
    taps = weight.reshape(3, 3, 3, chans, weight.shape[2])
    kflip = jnp.transpose(taps[::-1, ::-1, ::-1], (0, 1, 2, 4, 3))
    pad = [(0, 0), (0, 0), (1, 1)]
    inner = lax.conv_general_dilated(
        gh[None], kflip, (1, 1, 1), pad,
        dimension_numbers=("NDHWC", "DHWIO", "NDHWC"),
        preferred_element_type=jnp.float32,
    )[0]
    grad_in = inner.astype(jnp.bfloat16)
    gshare = lax.dynamic_slice_in_dim(gh, offset, half, 3)
    gdeep = jnp.pad(gshare, ((0, 0), (0, 0), (1, 1), (0, 0)))
    shifted = jnp.concatenate(
        [
            gdeep[2 - a : 2 - a + size_x, 2 - b : 2 - b + size_y, 2 - c : 2 - c + depth]
            for a in range(3)
            for b in range(3)
            for c in range(3)
        ],
        axis=3,
    )
    term = lax.dot_general(
        x_act, shifted, (((0, 1, 2), (0, 1, 2)), ((), ())), preferred_element_type=jnp.float32
    )
    weight_terms = jnp.transpose(term.reshape(chans, 27, half), (1, 0, 2)).reshape(27 * chans, half)
    nx = lax.axis_size("gx")
    ny = lax.axis_size("gy")
    blocks = weight_terms.reshape(nx, ny, weight_terms.shape[0] // (nx * ny), half)
    owned = scatter_sum(scatter_sum(blocks, "gy", 1), "gx", 0)
    total_cells = size_x * lax.axis_size("gx") * size_y * lax.axis_size("gy") * depth
    grad_weight = owned / jnp.sqrt(jnp.float32(total_cells))
    return (grad_in, grad_weight)


def solution(mesh):
    return jax.shard_map(
        on_device,
        mesh=mesh,
        in_specs=(P(("grp", "gx"), "gy", None, None), P(("grp", "gx"), "gy", None, None), P()),
        out_specs=(P(("grp", "gx"), "gy", None, None), P(("grp", "gx", "gy"), "col")),
        check_vma=False,
    )
```

```python
import jax
import jax.numpy as jnp
from jax import lax
from jax.sharding import PartitionSpec as P


def with_halo(cells, sides, width):
    for axis, dim in sides:
        count = lax.axis_size(axis)
        head = lax.slice_in_dim(cells, 0, width, axis=dim)
        tail = lax.slice_in_dim(cells, cells.shape[dim] - width, cells.shape[dim], axis=dim)
        if count == 1:
            low = jnp.zeros_like(tail)
            high = jnp.zeros_like(head)
        elif count == 2:
            me = lax.axis_index(axis)
            got = lax.ppermute(jnp.where(me == 0, tail, head), axis, [(0, 1), (1, 0)])
            low = jnp.where(me == 1, got, jnp.zeros_like(got))
            high = jnp.where(me == 0, got, jnp.zeros_like(got))
        else:
            low = lax.ppermute(tail, axis, [(i, i + 1) for i in range(count - 1)])
            high = lax.ppermute(head, axis, [(i + 1, i) for i in range(count - 1)])
        cells = jnp.concatenate([low, cells, high], axis=dim)
    return cells


def scatter_sum(blocks, axis, dim):
    count = lax.axis_size(axis)
    if count == 1:
        return lax.index_in_dim(blocks, 0, dim, keepdims=False)
    if count > 4:
        return lax.psum_scatter(blocks, axis, scatter_dimension=dim, tiled=False)
    me = lax.axis_index(axis)
    total = lax.dynamic_index_in_dim(blocks, me, dim, keepdims=False)
    for shift in range(1, count):
        part = lax.dynamic_index_in_dim(blocks, (me + shift) % count, dim, keepdims=False)
        total = total + lax.ppermute(part, axis, [(j, (j + shift) % count) for j in range(count)])
    return total


def take_rows(pieces, start, count):
    step = pieces[0].shape[0]
    out = []
    row = start
    while row < start + count:
        at = row % step
        take = min(start + count - row, step - at)
        out.append(pieces[row // step][at : at + take])
        row += take
    return jnp.concatenate(out, axis=0) if len(out) > 1 else out[0]


def on_device(x_act, grad_out, weight):
    size_x, size_y, depth, chans = x_act.shape
    ncores = lax.axis_size("col")
    half = weight.shape[2] // ncores
    offset = lax.axis_index("col") * half
    gh = with_halo(grad_out, (("gy", 1), ("gx", 0)), 1)
    taps = weight.reshape(3, 3, 3, chans, weight.shape[2])
    kflip = jnp.transpose(taps[::-1, ::-1, ::-1], (0, 1, 2, 4, 3))
    pad = [(0, 0), (0, 0), (1, 1)]
    inner = lax.conv_general_dilated(
        gh[None], kflip, (1, 1, 1), pad,
        dimension_numbers=("NDHWC", "DHWIO", "NDHWC"),
        preferred_element_type=jnp.float32,
    )[0]
    grad_in = inner.astype(jnp.bfloat16)
    gshare = lax.dynamic_slice_in_dim(gh, offset, half, 3)
    gdeep = jnp.pad(gshare, ((0, 0), (0, 0), (1, 1), (0, 0)))
    stack = jnp.concatenate([lax.slice_in_dim(gdeep, 2 - c, 2 - c + depth, axis=2) for c in range(3)], axis=3)
    pieces = []
    for a in range(3):
        for b in range(3):
            window = stack[2 - a : 2 - a + size_x, 2 - b : 2 - b + size_y]
            term = lax.dot_general(
                x_act, window, (((0, 1, 2), (0, 1, 2)), ((), ())), preferred_element_type=jnp.float32
            )
            pieces.append(jnp.transpose(term.reshape(chans, 3, half), (1, 0, 2)).reshape(3 * chans, half))
    nx = lax.axis_size("gx")
    ny = lax.axis_size("gy")
    owned_rows = 27 * chans // (nx * ny)
    if ny == 2:
        iy = lax.axis_index("gy")
        side = [
            jnp.stack([take_rows(pieces, (gx * 2 + y) * owned_rows, owned_rows) for gx in range(nx)])
            for y in range(2)
        ]
        keep = jnp.where(iy == 0, side[0], side[1])
        send = jnp.where(iy == 0, side[1], side[0])
        partial = keep + lax.ppermute(send, "gy", [(0, 1), (1, 0)])
    else:
        weight_terms = jnp.concatenate(pieces, axis=0)
        blocks = weight_terms.reshape(nx, ny, owned_rows, half)
        partial = scatter_sum(blocks, "gy", 1)
    owned = scatter_sum(partial, "gx", 0)
    total_cells = size_x * lax.axis_size("gx") * size_y * lax.axis_size("gy") * depth
    grad_weight = owned / jnp.sqrt(jnp.float32(total_cells))
    return (grad_in, grad_weight)


def solution(mesh):
    return jax.shard_map(
        on_device,
        mesh=mesh,
        in_specs=(P(("grp", "gx"), "gy", None, None), P(("grp", "gx"), "gy", None, None), P()),
        out_specs=(P(("grp", "gx"), "gy", None, None), P(("grp", "gx", "gy"), "col")),
        check_vma=False,
    )
```

```python
import jax
import jax.numpy as jnp
from jax import lax
from jax.sharding import PartitionSpec as P


def with_halo(cells, sides, width):
    for axis, dim in sides:
        count = lax.axis_size(axis)
        head = lax.slice_in_dim(cells, 0, width, axis=dim)
        tail = lax.slice_in_dim(cells, cells.shape[dim] - width, cells.shape[dim], axis=dim)
        if count == 1:
            low = jnp.zeros_like(tail)
            high = jnp.zeros_like(head)
        elif count == 2:
            me = lax.axis_index(axis)
            got = lax.ppermute(jnp.where(me == 0, tail, head), axis, [(0, 1), (1, 0)])
            low = jnp.where(me == 1, got, jnp.zeros_like(got))
            high = jnp.where(me == 0, got, jnp.zeros_like(got))
        else:
            me = lax.axis_index(axis)
            low = lax.ppermute(tail, axis, [(i, (i + 1) % count) for i in range(count)])
            high = lax.ppermute(head, axis, [((i + 1) % count, i) for i in range(count)])
            low = jnp.where(me == 0, jnp.zeros_like(low), low)
            high = jnp.where(me == count - 1, jnp.zeros_like(high), high)
        cells = jnp.concatenate([low, cells, high], axis=dim)
    return cells


def scatter_sum(blocks, axis, dim):
    count = lax.axis_size(axis)
    if count == 1:
        return lax.index_in_dim(blocks, 0, dim, keepdims=False)
    if count > 4:
        return lax.psum_scatter(blocks, axis, scatter_dimension=dim, tiled=False)
    me = lax.axis_index(axis)
    total = lax.dynamic_index_in_dim(blocks, me, dim, keepdims=False)
    for shift in range(1, count):
        part = lax.dynamic_index_in_dim(blocks, (me + shift) % count, dim, keepdims=False)
        total = total + lax.ppermute(part, axis, [(j, (j + shift) % count) for j in range(count)])
    return total


def take_rows(pieces, start, count):
    step = pieces[0].shape[0]
    out = []
    row = start
    while row < start + count:
        at = row % step
        take = min(start + count - row, step - at)
        out.append(pieces[row // step][at : at + take])
        row += take
    return jnp.concatenate(out, axis=0) if len(out) > 1 else out[0]


def on_device(x_act, grad_out, weight):
    size_x, size_y, depth, chans = x_act.shape
    ncores = lax.axis_size("col")
    half = weight.shape[2] // ncores
    offset = lax.axis_index("col") * half
    gh = with_halo(grad_out, (("gy", 1), ("gx", 0)), 1)
    taps = weight.reshape(3, 3, 3, chans, weight.shape[2])
    kflip = jnp.transpose(taps[::-1, ::-1, ::-1], (0, 1, 2, 4, 3))
    pad = [(0, 0), (0, 0), (1, 1)]
    inner = lax.conv_general_dilated(
        gh[None], kflip, (1, 1, 1), pad,
        dimension_numbers=("NDHWC", "DHWIO", "NDHWC"),
        preferred_element_type=jnp.float32,
    )[0]
    grad_in = inner.astype(jnp.bfloat16)
    gshare = lax.dynamic_slice_in_dim(gh, offset, half, 3)
    gdeep = jnp.pad(gshare, ((0, 0), (0, 0), (1, 1), (0, 0)))
    stack = jnp.concatenate([lax.slice_in_dim(gdeep, 2 - c, 2 - c + depth, axis=2) for c in range(3)], axis=3)
    pieces = []
    for a in range(3):
        for b in range(3):
            window = stack[2 - a : 2 - a + size_x, 2 - b : 2 - b + size_y]
            term = lax.dot_general(
                x_act, window, (((0, 1, 2), (0, 1, 2)), ((), ())), preferred_element_type=jnp.float32
            )
            pieces.append(jnp.transpose(term.reshape(chans, 3, half), (1, 0, 2)).reshape(3 * chans, half))
    nx = lax.axis_size("gx")
    ny = lax.axis_size("gy")
    owned_rows = 27 * chans // (nx * ny)
    if ny == 2:
        iy = lax.axis_index("gy")
        side = [
            jnp.stack([take_rows(pieces, (gx * 2 + y) * owned_rows, owned_rows) for gx in range(nx)])
            for y in range(2)
        ]
        keep = jnp.where(iy == 0, side[0], side[1])
        send = jnp.where(iy == 0, side[1], side[0])
        partial = keep + lax.ppermute(send, "gy", [(0, 1), (1, 0)])
    else:
        weight_terms = jnp.concatenate(pieces, axis=0)
        blocks = weight_terms.reshape(nx, ny, owned_rows, half)
        partial = scatter_sum(blocks, "gy", 1)
    owned = scatter_sum(partial, "gx", 0)
    total_cells = size_x * lax.axis_size("gx") * size_y * lax.axis_size("gy") * depth
    grad_weight = owned / jnp.sqrt(jnp.float32(total_cells))
    return (grad_in, grad_weight)


def solution(mesh):
    return jax.shard_map(
        on_device,
        mesh=mesh,
        in_specs=(P(("grp", "gx"), "gy", None, None), P(("grp", "gx"), "gy", None, None), P()),
        out_specs=(P(("grp", "gx"), "gy", None, None), P(("grp", "gx", "gy"), "col")),
        check_vma=False,
    )
```

```python
import jax
import jax.numpy as jnp
from jax import lax
from jax.sharding import PartitionSpec as P


def with_halo(cells, sides, width):
    for axis, dim in sides:
        count = lax.axis_size(axis)
        head = lax.slice_in_dim(cells, 0, width, axis=dim)
        tail = lax.slice_in_dim(cells, cells.shape[dim] - width, cells.shape[dim], axis=dim)
        if count == 1:
            low = jnp.zeros_like(tail)
            high = jnp.zeros_like(head)
        elif count == 2:
            me = lax.axis_index(axis)
            got = lax.ppermute(jnp.where(me == 0, tail, head), axis, [(0, 1), (1, 0)])
            low = jnp.where(me == 1, got, jnp.zeros_like(got))
            high = jnp.where(me == 0, got, jnp.zeros_like(got))
        else:
            me = lax.axis_index(axis)
            low = lax.ppermute(tail, axis, [(i, (i + 1) % count) for i in range(count)])
            high = lax.ppermute(head, axis, [((i + 1) % count, i) for i in range(count)])
            low = jnp.where(me == 0, jnp.zeros_like(low), low)
            high = jnp.where(me == count - 1, jnp.zeros_like(high), high)
        cells = jnp.concatenate([low, cells, high], axis=dim)
    return cells


def scatter_sum(blocks, axis, dim):
    count = lax.axis_size(axis)
    if count == 1:
        return lax.index_in_dim(blocks, 0, dim, keepdims=False)
    if count > 4:
        return lax.psum_scatter(blocks, axis, scatter_dimension=dim, tiled=False)
    me = lax.axis_index(axis)
    total = lax.dynamic_index_in_dim(blocks, me, dim, keepdims=False)
    for shift in range(1, count):
        part = lax.dynamic_index_in_dim(blocks, (me + shift) % count, dim, keepdims=False)
        total = total + lax.ppermute(part, axis, [(j, (j + shift) % count) for j in range(count)])
    return total


def take_rows(pieces, start, count):
    step = pieces[0].shape[0]
    out = []
    row = start
    while row < start + count:
        at = row % step
        take = min(start + count - row, step - at)
        out.append(pieces[row // step][at : at + take])
        row += take
    return jnp.concatenate(out, axis=0) if len(out) > 1 else out[0]


def on_device(x_act, grad_out, weight):
    size_x, size_y, depth, chans = x_act.shape
    ncores = lax.axis_size("col")
    half = weight.shape[2] // ncores
    offset = lax.axis_index("col") * half
    gh = with_halo(grad_out, (("gy", 1), ("gx", 0)), 1)
    taps = weight.reshape(3, 3, 3, chans, weight.shape[2])
    kflip = jnp.transpose(taps[::-1, ::-1, ::-1], (0, 1, 2, 4, 3))
    pad = [(0, 0), (0, 0), (1, 1)]
    inner = lax.conv_general_dilated(
        gh[None], kflip, (1, 1, 1), pad,
        dimension_numbers=("NDHWC", "DHWIO", "NDHWC"),
        preferred_element_type=jnp.float32,
    )[0]
    grad_in = inner.astype(jnp.bfloat16)
    gshare = lax.dynamic_slice_in_dim(gh, offset, half, 3)
    gdeep = jnp.pad(gshare, ((0, 0), (0, 0), (1, 1), (0, 0)))
    stack = jnp.concatenate([lax.slice_in_dim(gdeep, 2 - c, 2 - c + depth, axis=2) for c in range(3)], axis=3)
    pieces = []
    for a in range(3):
        for b in range(3):
            window = stack[2 - a : 2 - a + size_x, 2 - b : 2 - b + size_y]
            term = lax.dot_general(
                x_act, window, (((0, 1, 2), (0, 1, 2)), ((), ())), preferred_element_type=jnp.float32
            )
            pieces.append(jnp.transpose(term.reshape(chans, 3, half), (1, 0, 2)).reshape(3 * chans, half))
    nx = lax.axis_size("gx")
    ny = lax.axis_size("gy")
    owned_rows = 27 * chans // (nx * ny)
    if ny == 2:
        iy = lax.axis_index("gy")
        side = [
            jnp.stack([take_rows(pieces, (gx * 2 + y) * owned_rows, owned_rows) for gx in range(nx)])
            for y in range(2)
        ]
        split = owned_rows // 2 if owned_rows % 16 == 0 else owned_rows
        parts = []
        for lo, hi in ((0, split), (split, owned_rows)):
            if lo == hi:
                continue
            keep = jnp.where(iy == 0, side[0][:, lo:hi], side[1][:, lo:hi])
            send = jnp.where(iy == 0, side[1][:, lo:hi], side[0][:, lo:hi])
            partial = keep + lax.ppermute(send, "gy", [(0, 1), (1, 0)])
            parts.append(scatter_sum(partial, "gx", 0))
        owned = jnp.concatenate(parts, axis=0) if len(parts) > 1 else parts[0]
    else:
        weight_terms = jnp.concatenate(pieces, axis=0)
        blocks = weight_terms.reshape(nx, ny, owned_rows, half)
        owned = scatter_sum(scatter_sum(blocks, "gy", 1), "gx", 0)
    total_cells = size_x * lax.axis_size("gx") * size_y * lax.axis_size("gy") * depth
    grad_weight = owned / jnp.sqrt(jnp.float32(total_cells))
    return (grad_in, grad_weight)


def solution(mesh):
    return jax.shard_map(
        on_device,
        mesh=mesh,
        in_specs=(P(("grp", "gx"), "gy", None, None), P(("grp", "gx"), "gy", None, None), P()),
        out_specs=(P(("grp", "gx"), "gy", None, None), P(("grp", "gx", "gy"), "col")),
        check_vma=False,
    )
```

```python
import jax
import jax.numpy as jnp
from jax import lax
from jax.sharding import PartitionSpec as P


def with_halo(cells, sides, width):
    for axis, dim in sides:
        count = lax.axis_size(axis)
        head = lax.slice_in_dim(cells, 0, width, axis=dim)
        tail = lax.slice_in_dim(cells, cells.shape[dim] - width, cells.shape[dim], axis=dim)
        if count == 1:
            low = jnp.zeros_like(tail)
            high = jnp.zeros_like(head)
        elif count == 2:
            me = lax.axis_index(axis)
            got = lax.ppermute(jnp.where(me == 0, tail, head), axis, [(0, 1), (1, 0)])
            low = jnp.where(me == 1, got, jnp.zeros_like(got))
            high = jnp.where(me == 0, got, jnp.zeros_like(got))
        else:
            me = lax.axis_index(axis)
            low = lax.ppermute(tail, axis, [(i, (i + 1) % count) for i in range(count)])
            high = lax.ppermute(head, axis, [((i + 1) % count, i) for i in range(count)])
            low = jnp.where(me == 0, jnp.zeros_like(low), low)
            high = jnp.where(me == count - 1, jnp.zeros_like(high), high)
        cells = jnp.concatenate([low, cells, high], axis=dim)
    return cells


def scatter_sum(blocks, axis, dim):
    count = lax.axis_size(axis)
    if count == 1:
        return lax.index_in_dim(blocks, 0, dim, keepdims=False)
    if count > 4:
        return lax.psum_scatter(blocks, axis, scatter_dimension=dim, tiled=False)
    me = lax.axis_index(axis)
    total = lax.dynamic_index_in_dim(blocks, me, dim, keepdims=False)
    for shift in range(1, count):
        part = lax.dynamic_index_in_dim(blocks, (me + shift) % count, dim, keepdims=False)
        total = total + lax.ppermute(part, axis, [(j, (j + shift) % count) for j in range(count)])
    return total


def take_rows(pieces, start, count):
    step = pieces[0].shape[0]
    out = []
    row = start
    while row < start + count:
        at = row % step
        take = min(start + count - row, step - at)
        out.append(pieces[row // step][at : at + take])
        row += take
    return jnp.concatenate(out, axis=0) if len(out) > 1 else out[0]


def on_device(x_act, grad_out, weight):
    size_x, size_y, depth, chans = x_act.shape
    ncores = lax.axis_size("col")
    half = weight.shape[2] // ncores
    offset = lax.axis_index("col") * half
    gh = with_halo(grad_out, (("gy", 1), ("gx", 0)), 1)
    taps = weight.reshape(3, 3, 3, chans, weight.shape[2])
    kflip = jnp.transpose(taps[::-1, ::-1, ::-1], (0, 1, 2, 4, 3))
    pad = [(0, 0), (0, 0), (1, 1)]
    gshare = lax.dynamic_slice_in_dim(gh, offset, half, 3)
    gdeep = jnp.pad(gshare, ((0, 0), (0, 0), (1, 1), (0, 0)))
    stack = jnp.concatenate([lax.slice_in_dim(gdeep, 2 - c, 2 - c + depth, axis=2) for c in range(3)], axis=3)
    pieces = []
    for a in range(3):
        for b in range(3):
            window = stack[2 - a : 2 - a + size_x, 2 - b : 2 - b + size_y]
            term = lax.dot_general(
                x_act, window, (((0, 1, 2), (0, 1, 2)), ((), ())), preferred_element_type=jnp.float32
            )
            pieces.append(jnp.transpose(term.reshape(chans, 3, half), (1, 0, 2)).reshape(3 * chans, half))
    nx = lax.axis_size("gx")
    ny = lax.axis_size("gy")
    owned_rows = 27 * chans // (nx * ny)
    gates = []
    if ny == 2:
        iy = lax.axis_index("gy")
        side = [
            jnp.stack([take_rows(pieces, (gx * 2 + y) * owned_rows, owned_rows) for gx in range(nx)])
            for y in range(2)
        ]
        split = owned_rows // 2 if owned_rows % 16 == 0 else owned_rows
        partials = []
        for lo, hi in ((0, split), (split, owned_rows)):
            if lo == hi:
                continue
            keep = jnp.where(iy == 0, side[0][:, lo:hi], side[1][:, lo:hi])
            send = jnp.where(iy == 0, side[1][:, lo:hi], side[0][:, lo:hi])
            partials.append(keep + lax.ppermute(send, "gy", [(0, 1), (1, 0)]))
        gates = partials
        parts = [scatter_sum(partial, "gx", 0) for partial in partials]
        owned = jnp.concatenate(parts, axis=0) if len(parts) > 1 else parts[0]
    else:
        weight_terms = jnp.concatenate(pieces, axis=0)
        blocks = weight_terms.reshape(nx, ny, owned_rows, half)
        owned = scatter_sum(scatter_sum(blocks, "gy", 1), "gx", 0)
    if gates:
        gh = lax.optimization_barrier((gh, *gates))[0]
    inner = lax.conv_general_dilated(
        gh[None], kflip, (1, 1, 1), pad,
        dimension_numbers=("NDHWC", "DHWIO", "NDHWC"),
        preferred_element_type=jnp.float32,
    )[0]
    grad_in = inner.astype(jnp.bfloat16)
    total_cells = size_x * lax.axis_size("gx") * size_y * lax.axis_size("gy") * depth
    grad_weight = owned / jnp.sqrt(jnp.float32(total_cells))
    return (grad_in, grad_weight)


def solution(mesh):
    return jax.shard_map(
        on_device,
        mesh=mesh,
        in_specs=(P(("grp", "gx"), "gy", None, None), P(("grp", "gx"), "gy", None, None), P()),
        out_specs=(P(("grp", "gx"), "gy", None, None), P(("grp", "gx", "gy"), "col")),
        check_vma=False,
    )
```

```python
import jax
import jax.numpy as jnp
from jax import lax
from jax.sharding import PartitionSpec as P


def with_halo(cells, sides, width):
    for axis, dim in sides:
        count = lax.axis_size(axis)
        head = lax.slice_in_dim(cells, 0, width, axis=dim)
        tail = lax.slice_in_dim(cells, cells.shape[dim] - width, cells.shape[dim], axis=dim)
        if count == 1:
            low = jnp.zeros_like(tail)
            high = jnp.zeros_like(head)
        elif count == 2:
            me = lax.axis_index(axis)
            got = lax.ppermute(jnp.where(me == 0, tail, head), axis, [(0, 1), (1, 0)])
            low = jnp.where(me == 1, got, jnp.zeros_like(got))
            high = jnp.where(me == 0, got, jnp.zeros_like(got))
        else:
            me = lax.axis_index(axis)
            low = lax.ppermute(tail, axis, [(i, (i + 1) % count) for i in range(count)])
            high = lax.ppermute(head, axis, [((i + 1) % count, i) for i in range(count)])
            low = jnp.where(me == 0, jnp.zeros_like(low), low)
            high = jnp.where(me == count - 1, jnp.zeros_like(high), high)
        cells = jnp.concatenate([low, cells, high], axis=dim)
    return cells


def scatter_sum(blocks, axis, dim):
    count = lax.axis_size(axis)
    if count == 1:
        return lax.index_in_dim(blocks, 0, dim, keepdims=False)
    if count > 4:
        return lax.psum_scatter(blocks, axis, scatter_dimension=dim, tiled=False)
    me = lax.axis_index(axis)
    total = lax.dynamic_index_in_dim(blocks, me, dim, keepdims=False)
    for shift in range(1, count):
        part = lax.dynamic_index_in_dim(blocks, (me + shift) % count, dim, keepdims=False)
        total = total + lax.ppermute(part, axis, [(j, (j + shift) % count) for j in range(count)])
    return total


def take_rows(pieces, start, count):
    step = pieces[0].shape[0]
    out = []
    row = start
    while row < start + count:
        at = row % step
        take = min(start + count - row, step - at)
        out.append(pieces[row // step][at : at + take])
        row += take
    return jnp.concatenate(out, axis=0) if len(out) > 1 else out[0]


def on_device(x_act, grad_out, weight):
    size_x, size_y, depth, chans = x_act.shape
    ncores = lax.axis_size("col")
    half = weight.shape[2] // ncores
    offset = lax.axis_index("col") * half
    widened = with_halo(grad_out, (("gy", 1),), 1)
    gh = with_halo(widened, (("gx", 0),), 1)
    taps = weight.reshape(3, 3, 3, chans, weight.shape[2])
    kflip = jnp.transpose(taps[::-1, ::-1, ::-1], (0, 1, 2, 4, 3))
    pad = [(0, 0), (0, 0), (1, 1)]
    inner = lax.conv_general_dilated(
        gh[None], kflip, (1, 1, 1), pad,
        dimension_numbers=("NDHWC", "DHWIO", "NDHWC"),
        preferred_element_type=jnp.float32,
    )[0]
    grad_in = inner.astype(jnp.bfloat16)

    def depth_stack(cells):
        deep = jnp.pad(cells, ((0, 0), (0, 0), (1, 1), (0, 0)))
        return jnp.concatenate([lax.slice_in_dim(deep, 2 - c, 2 - c + depth, axis=2) for c in range(3)], axis=3)

    def contract(xs, ws):
        return lax.dot_general(xs, ws, (((0, 1, 2), (0, 1, 2)), ((), ())), preferred_element_type=jnp.float32)

    local = depth_stack(lax.dynamic_slice_in_dim(widened, offset, half, 3))
    gshare = lax.dynamic_slice_in_dim(gh, offset, half, 3)
    below = depth_stack(gshare[:1])
    above = depth_stack(gshare[size_x + 1 :])
    pieces = []
    for a in range(3):
        for b in range(3):
            cols = slice(2 - b, 2 - b + size_y)
            if a == 1:
                term = contract(x_act, local[:, cols])
            elif a == 0:
                term = contract(x_act[: size_x - 1], local[1:, cols]) + contract(x_act[size_x - 1 :], above[:, cols])
            else:
                term = contract(x_act[1:], local[: size_x - 1, cols]) + contract(x_act[:1], below[:, cols])
            pieces.append(jnp.transpose(term.reshape(chans, 3, half), (1, 0, 2)).reshape(3 * chans, half))
    nx = lax.axis_size("gx")
    ny = lax.axis_size("gy")
    owned_rows = 27 * chans // (nx * ny)
    if ny == 2:
        iy = lax.axis_index("gy")
        side = [
            jnp.stack([take_rows(pieces, (gx * 2 + y) * owned_rows, owned_rows) for gx in range(nx)])
            for y in range(2)
        ]
        split = owned_rows // 2 if owned_rows % 16 == 0 else owned_rows
        parts = []
        for lo, hi in ((0, split), (split, owned_rows)):
            if lo == hi:
                continue
            keep = jnp.where(iy == 0, side[0][:, lo:hi], side[1][:, lo:hi])
            send = jnp.where(iy == 0, side[1][:, lo:hi], side[0][:, lo:hi])
            partial = keep + lax.ppermute(send, "gy", [(0, 1), (1, 0)])
            parts.append(scatter_sum(partial, "gx", 0))
        owned = jnp.concatenate(parts, axis=0) if len(parts) > 1 else parts[0]
    else:
        weight_terms = jnp.concatenate(pieces, axis=0)
        blocks = weight_terms.reshape(nx, ny, owned_rows, half)
        owned = scatter_sum(scatter_sum(blocks, "gy", 1), "gx", 0)
    total_cells = size_x * lax.axis_size("gx") * size_y * lax.axis_size("gy") * depth
    grad_weight = owned / jnp.sqrt(jnp.float32(total_cells))
    return (grad_in, grad_weight)


def solution(mesh):
    return jax.shard_map(
        on_device,
        mesh=mesh,
        in_specs=(P(("grp", "gx"), "gy", None, None), P(("grp", "gx"), "gy", None, None), P()),
        out_specs=(P(("grp", "gx"), "gy", None, None), P(("grp", "gx", "gy"), "col")),
        check_vma=False,
    )
```

```python
import jax
import jax.numpy as jnp
from jax import lax
from jax.sharding import PartitionSpec as P


def with_halo(cells, sides, width):
    for axis, dim in sides:
        count = lax.axis_size(axis)
        head = lax.slice_in_dim(cells, 0, width, axis=dim)
        tail = lax.slice_in_dim(cells, cells.shape[dim] - width, cells.shape[dim], axis=dim)
        if count == 1:
            low = jnp.zeros_like(tail)
            high = jnp.zeros_like(head)
        elif count == 2:
            me = lax.axis_index(axis)
            got = lax.ppermute(jnp.where(me == 0, tail, head), axis, [(0, 1), (1, 0)])
            low = jnp.where(me == 1, got, jnp.zeros_like(got))
            high = jnp.where(me == 0, got, jnp.zeros_like(got))
        else:
            me = lax.axis_index(axis)
            low = lax.ppermute(tail, axis, [(i, (i + 1) % count) for i in range(count)])
            high = lax.ppermute(head, axis, [((i + 1) % count, i) for i in range(count)])
            low = jnp.where(me == 0, jnp.zeros_like(low), low)
            high = jnp.where(me == count - 1, jnp.zeros_like(high), high)
        cells = jnp.concatenate([low, cells, high], axis=dim)
    return cells


def scatter_sum(blocks, axis, dim):
    count = lax.axis_size(axis)
    if count == 1:
        return lax.index_in_dim(blocks, 0, dim, keepdims=False)
    if count > 4:
        return lax.psum_scatter(blocks, axis, scatter_dimension=dim, tiled=False)
    me = lax.axis_index(axis)
    total = lax.dynamic_index_in_dim(blocks, me, dim, keepdims=False)
    for shift in range(1, count):
        part = lax.dynamic_index_in_dim(blocks, (me + shift) % count, dim, keepdims=False)
        total = total + lax.ppermute(part, axis, [(j, (j + shift) % count) for j in range(count)])
    return total


def take_rows(pieces, start, count):
    step = pieces[0].shape[0]
    out = []
    row = start
    while row < start + count:
        at = row % step
        take = min(start + count - row, step - at)
        out.append(pieces[row // step][at : at + take])
        row += take
    return jnp.concatenate(out, axis=0) if len(out) > 1 else out[0]


def on_device(x_act, grad_out, weight):
    size_x, size_y, depth, chans = x_act.shape
    ncores = lax.axis_size("col")
    half = weight.shape[2] // ncores
    offset = lax.axis_index("col") * half
    gh = with_halo(grad_out, (("gy", 1), ("gx", 0)), 1)
    taps = weight.reshape(3, 3, 3, chans, weight.shape[2])
    kflip = jnp.transpose(taps[::-1, ::-1, ::-1], (0, 1, 2, 4, 3))
    pad = [(0, 0), (0, 0), (1, 1)]
    gshare = lax.dynamic_slice_in_dim(gh, offset, half, 3)
    gdeep = jnp.pad(gshare, ((0, 0), (0, 0), (1, 1), (0, 0)))
    stack = jnp.concatenate([lax.slice_in_dim(gdeep, 2 - c, 2 - c + depth, axis=2) for c in range(3)], axis=3)
    pieces = []
    for a in range(3):
        for b in range(3):
            window = stack[2 - a : 2 - a + size_x, 2 - b : 2 - b + size_y]
            term = lax.dot_general(
                x_act, window, (((0, 1, 2), (0, 1, 2)), ((), ())), preferred_element_type=jnp.float32
            )
            pieces.append(jnp.transpose(term.reshape(chans, 3, half), (1, 0, 2)).reshape(3 * chans, half))
    nx = lax.axis_size("gx")
    ny = lax.axis_size("gy")
    owned_rows = 27 * chans // (nx * ny)
    gates = []
    if ny == 2:
        iy = lax.axis_index("gy")
        side = [
            jnp.stack([take_rows(pieces, (gx * 2 + y) * owned_rows, owned_rows) for gx in range(nx)])
            for y in range(2)
        ]
        split = owned_rows // 2 if owned_rows % 16 == 0 else owned_rows
        parts = []
        for lo, hi in ((0, split), (split, owned_rows)):
            if lo == hi:
                continue
            keep = jnp.where(iy == 0, side[0][:, lo:hi], side[1][:, lo:hi])
            send = jnp.where(iy == 0, side[1][:, lo:hi], side[0][:, lo:hi])
            partial = keep + lax.ppermute(send, "gy", [(0, 1), (1, 0)])
            gates.append(partial)
            parts.append(scatter_sum(partial, "gx", 0))
        owned = jnp.concatenate(parts, axis=0) if len(parts) > 1 else parts[0]
    else:
        weight_terms = jnp.concatenate(pieces, axis=0)
        blocks = weight_terms.reshape(nx, ny, owned_rows, half)
        owned = scatter_sum(scatter_sum(blocks, "gy", 1), "gx", 0)
    rows = size_x // 2 if size_x % 2 == 0 else size_x
    halves = []
    for lo in range(0, size_x, rows):
        source = gh
        if lo > 0 and gates:
            source = lax.optimization_barrier((gh, gates[0]))[0]
        halves.append(
            lax.conv_general_dilated(
                source[None, lo : lo + rows + 2], kflip, (1, 1, 1), pad,
                dimension_numbers=("NDHWC", "DHWIO", "NDHWC"),
                preferred_element_type=jnp.float32,
            )[0].astype(jnp.bfloat16)
        )
    grad_in = jnp.concatenate(halves, axis=0) if len(halves) > 1 else halves[0]
    total_cells = size_x * lax.axis_size("gx") * size_y * lax.axis_size("gy") * depth
    grad_weight = owned / jnp.sqrt(jnp.float32(total_cells))
    return (grad_in, grad_weight)


def solution(mesh):
    return jax.shard_map(
        on_device,
        mesh=mesh,
        in_specs=(P(("grp", "gx"), "gy", None, None), P(("grp", "gx"), "gy", None, None), P()),
        out_specs=(P(("grp", "gx"), "gy", None, None), P(("grp", "gx", "gy"), "col")),
        check_vma=False,
    )
```

```python
import jax
import jax.numpy as jnp
from jax import lax
from jax.sharding import PartitionSpec as P


def with_halo(cells, sides, width):
    for axis, dim in sides:
        count = lax.axis_size(axis)
        head = lax.slice_in_dim(cells, 0, width, axis=dim)
        tail = lax.slice_in_dim(cells, cells.shape[dim] - width, cells.shape[dim], axis=dim)
        if count == 1:
            low = jnp.zeros_like(tail)
            high = jnp.zeros_like(head)
        elif count == 2:
            me = lax.axis_index(axis)
            got = lax.ppermute(jnp.where(me == 0, tail, head), axis, [(0, 1), (1, 0)])
            low = jnp.where(me == 1, got, jnp.zeros_like(got))
            high = jnp.where(me == 0, got, jnp.zeros_like(got))
        else:
            me = lax.axis_index(axis)
            low = lax.ppermute(tail, axis, [(i, (i + 1) % count) for i in range(count)])
            high = lax.ppermute(head, axis, [((i + 1) % count, i) for i in range(count)])
            low = jnp.where(me == 0, jnp.zeros_like(low), low)
            high = jnp.where(me == count - 1, jnp.zeros_like(high), high)
        cells = jnp.concatenate([low, cells, high], axis=dim)
    return cells


def scatter_sum(blocks, axis, dim):
    count = lax.axis_size(axis)
    if count == 1:
        return lax.index_in_dim(blocks, 0, dim, keepdims=False)
    if count > 4:
        return lax.psum_scatter(blocks, axis, scatter_dimension=dim, tiled=False)
    me = lax.axis_index(axis)
    total = lax.dynamic_index_in_dim(blocks, me, dim, keepdims=False)
    for shift in range(1, count):
        part = lax.dynamic_index_in_dim(blocks, (me + shift) % count, dim, keepdims=False)
        total = total + lax.ppermute(part, axis, [(j, (j + shift) % count) for j in range(count)])
    return total


def take_rows(pieces, start, count):
    step = pieces[0].shape[0]
    out = []
    row = start
    while row < start + count:
        at = row % step
        take = min(start + count - row, step - at)
        out.append(pieces[row // step][at : at + take])
        row += take
    return jnp.concatenate(out, axis=0) if len(out) > 1 else out[0]


def on_device(x_act, grad_out, weight):
    size_x, size_y, depth, chans = x_act.shape
    ncores = lax.axis_size("col")
    half = weight.shape[2] // ncores
    offset = lax.axis_index("col") * half
    gh = with_halo(grad_out, (("gy", 1), ("gx", 0)), 1)
    taps = weight.reshape(3, 3, 3, chans, weight.shape[2])
    kflip = jnp.transpose(taps[::-1, ::-1, ::-1], (0, 1, 2, 4, 3))
    pad = [(0, 0), (0, 0), (1, 1)]
    inner = lax.conv_general_dilated(
        gh[None], kflip, (1, 1, 1), pad,
        dimension_numbers=("NDHWC", "DHWIO", "NDHWC"),
        preferred_element_type=jnp.float32,
    )[0]
    grad_in = inner.astype(jnp.bfloat16)
    gshare = lax.dynamic_slice_in_dim(gh, offset, half, 3)
    gdeep = jnp.pad(gshare, ((0, 0), (0, 0), (1, 1), (0, 0)))
    stack = jnp.concatenate([lax.slice_in_dim(gdeep, 2 - c, 2 - c + depth, axis=2) for c in range(3)], axis=3)
    pieces = []
    for a in range(3):
        for b in range(3):
            window = stack[2 - a : 2 - a + size_x, 2 - b : 2 - b + size_y]
            term = lax.dot_general(
                x_act, window, (((0, 1, 2), (0, 1, 2)), ((), ())), preferred_element_type=jnp.float32
            )
            pieces.append(jnp.transpose(term.reshape(chans, 3, half), (1, 0, 2)).reshape(3 * chans, half))
    nx = lax.axis_size("gx")
    ny = lax.axis_size("gy")
    owned_rows = 27 * chans // (nx * ny)
    if ny == 2:
        iy = lax.axis_index("gy")
        side = [
            jnp.stack([take_rows(pieces, (gx * 2 + y) * owned_rows, owned_rows) for gx in range(nx)])
            for y in range(2)
        ]
        split = (owned_rows * 3 // 4) // 8 * 8 if owned_rows % 8 == 0 else owned_rows
        parts = []
        for lo, hi in ((0, split), (split, owned_rows)):
            if lo == hi:
                continue
            keep = jnp.where(iy == 0, side[0][:, lo:hi], side[1][:, lo:hi])
            send = jnp.where(iy == 0, side[1][:, lo:hi], side[0][:, lo:hi])
            partial = keep + lax.ppermute(send, "gy", [(0, 1), (1, 0)])
            parts.append(scatter_sum(partial, "gx", 0))
        owned = jnp.concatenate(parts, axis=0) if len(parts) > 1 else parts[0]
    else:
        weight_terms = jnp.concatenate(pieces, axis=0)
        blocks = weight_terms.reshape(nx, ny, owned_rows, half)
        owned = scatter_sum(scatter_sum(blocks, "gy", 1), "gx", 0)
    total_cells = size_x * lax.axis_size("gx") * size_y * lax.axis_size("gy") * depth
    grad_weight = owned / jnp.sqrt(jnp.float32(total_cells))
    return (grad_in, grad_weight)


def solution(mesh):
    return jax.shard_map(
        on_device,
        mesh=mesh,
        in_specs=(P(("grp", "gx"), "gy", None, None), P(("grp", "gx"), "gy", None, None), P()),
        out_specs=(P(("grp", "gx"), "gy", None, None), P(("grp", "gx", "gy"), "col")),
        check_vma=False,
    )
```

```python
import jax
import jax.numpy as jnp
from jax import lax
from jax.sharding import PartitionSpec as P


def with_halo(cells, sides, width):
    for axis, dim in sides:
        count = lax.axis_size(axis)
        head = lax.slice_in_dim(cells, 0, width, axis=dim)
        tail = lax.slice_in_dim(cells, cells.shape[dim] - width, cells.shape[dim], axis=dim)
        if count == 1:
            low = jnp.zeros_like(tail)
            high = jnp.zeros_like(head)
        elif count == 2:
            me = lax.axis_index(axis)
            got = lax.ppermute(jnp.where(me == 0, tail, head), axis, [(0, 1), (1, 0)])
            low = jnp.where(me == 1, got, jnp.zeros_like(got))
            high = jnp.where(me == 0, got, jnp.zeros_like(got))
        else:
            me = lax.axis_index(axis)
            low = lax.ppermute(tail, axis, [(i, (i + 1) % count) for i in range(count)])
            high = lax.ppermute(head, axis, [((i + 1) % count, i) for i in range(count)])
            low = jnp.where(me == 0, jnp.zeros_like(low), low)
            high = jnp.where(me == count - 1, jnp.zeros_like(high), high)
        cells = jnp.concatenate([low, cells, high], axis=dim)
    return cells


def scatter_sum(blocks, axis, dim):
    count = lax.axis_size(axis)
    if count == 1:
        return lax.index_in_dim(blocks, 0, dim, keepdims=False)
    if count > 4:
        return lax.psum_scatter(blocks, axis, scatter_dimension=dim, tiled=False)
    me = lax.axis_index(axis)
    total = lax.dynamic_index_in_dim(blocks, me, dim, keepdims=False)
    for shift in range(1, count):
        part = lax.dynamic_index_in_dim(blocks, (me + shift) % count, dim, keepdims=False)
        total = total + lax.ppermute(part, axis, [(j, (j + shift) % count) for j in range(count)])
    return total


def take_rows(pieces, start, count):
    step = pieces[0].shape[0]
    out = []
    row = start
    while row < start + count:
        at = row % step
        take = min(start + count - row, step - at)
        out.append(pieces[row // step][at : at + take])
        row += take
    return jnp.concatenate(out, axis=0) if len(out) > 1 else out[0]


def on_device(x_act, grad_out, weight):
    size_x, size_y, depth, chans = x_act.shape
    ncores = lax.axis_size("col")
    half = weight.shape[2] // ncores
    offset = lax.axis_index("col") * half
    gh = with_halo(grad_out, (("gy", 1), ("gx", 0)), 1)
    taps = weight.reshape(3, 3, 3, chans, weight.shape[2])
    kflip = jnp.transpose(taps[::-1, ::-1, ::-1], (0, 1, 2, 4, 3))
    pad = [(0, 0), (0, 0), (1, 1)]
    def conv_rows(source):
        return lax.conv_general_dilated(
            source[None], kflip, (1, 1, 1), pad,
            dimension_numbers=("NDHWC", "DHWIO", "NDHWC"),
            preferred_element_type=jnp.float32,
        )[0].astype(jnp.bfloat16)

    if ncores == 2 and size_x % 2 == 0:
        core = lax.axis_index("col")
        rows = size_x // 2
        mine = conv_rows(lax.dynamic_slice_in_dim(gh, core * rows, rows + 2, axis=0))
        other = lax.ppermute(mine, "col", [(0, 1), (1, 0)])
        grad_in = jnp.where(
            core == 0, jnp.concatenate([mine, other], axis=0), jnp.concatenate([other, mine], axis=0)
        )
    else:
        grad_in = conv_rows(gh)
    gshare = lax.dynamic_slice_in_dim(gh, offset, half, 3)
    gdeep = jnp.pad(gshare, ((0, 0), (0, 0), (1, 1), (0, 0)))
    stack = jnp.concatenate([lax.slice_in_dim(gdeep, 2 - c, 2 - c + depth, axis=2) for c in range(3)], axis=3)
    pieces = []
    for a in range(3):
        for b in range(3):
            window = stack[2 - a : 2 - a + size_x, 2 - b : 2 - b + size_y]
            term = lax.dot_general(
                x_act, window, (((0, 1, 2), (0, 1, 2)), ((), ())), preferred_element_type=jnp.float32
            )
            pieces.append(jnp.transpose(term.reshape(chans, 3, half), (1, 0, 2)).reshape(3 * chans, half))
    nx = lax.axis_size("gx")
    ny = lax.axis_size("gy")
    owned_rows = 27 * chans // (nx * ny)
    if ny == 2:
        iy = lax.axis_index("gy")
        side = [
            jnp.stack([take_rows(pieces, (gx * 2 + y) * owned_rows, owned_rows) for gx in range(nx)])
            for y in range(2)
        ]
        split = owned_rows // 2 if owned_rows % 16 == 0 else owned_rows
        parts = []
        for lo, hi in ((0, split), (split, owned_rows)):
            if lo == hi:
                continue
            keep = jnp.where(iy == 0, side[0][:, lo:hi], side[1][:, lo:hi])
            send = jnp.where(iy == 0, side[1][:, lo:hi], side[0][:, lo:hi])
            partial = keep + lax.ppermute(send, "gy", [(0, 1), (1, 0)])
            parts.append(scatter_sum(partial, "gx", 0))
        owned = jnp.concatenate(parts, axis=0) if len(parts) > 1 else parts[0]
    else:
        weight_terms = jnp.concatenate(pieces, axis=0)
        blocks = weight_terms.reshape(nx, ny, owned_rows, half)
        owned = scatter_sum(scatter_sum(blocks, "gy", 1), "gx", 0)
    total_cells = size_x * lax.axis_size("gx") * size_y * lax.axis_size("gy") * depth
    grad_weight = owned / jnp.sqrt(jnp.float32(total_cells))
    return (grad_in, grad_weight)


def solution(mesh):
    return jax.shard_map(
        on_device,
        mesh=mesh,
        in_specs=(P(("grp", "gx"), "gy", None, None), P(("grp", "gx"), "gy", None, None), P()),
        out_specs=(P(("grp", "gx"), "gy", None, None), P(("grp", "gx", "gy"), "col")),
        check_vma=False,
    )
```

```python
import jax
import jax.numpy as jnp
from jax import lax
from jax.sharding import PartitionSpec as P


def with_halo(cells, sides, width):
    for axis, dim in sides:
        count = lax.axis_size(axis)
        head = lax.slice_in_dim(cells, 0, width, axis=dim)
        tail = lax.slice_in_dim(cells, cells.shape[dim] - width, cells.shape[dim], axis=dim)
        if count == 1:
            low = jnp.zeros_like(tail)
            high = jnp.zeros_like(head)
        elif count == 2:
            me = lax.axis_index(axis)
            got = lax.ppermute(jnp.where(me == 0, tail, head), axis, [(0, 1), (1, 0)])
            low = jnp.where(me == 1, got, jnp.zeros_like(got))
            high = jnp.where(me == 0, got, jnp.zeros_like(got))
        else:
            me = lax.axis_index(axis)
            low = lax.ppermute(tail, axis, [(i, (i + 1) % count) for i in range(count)])
            high = lax.ppermute(head, axis, [((i + 1) % count, i) for i in range(count)])
            low = jnp.where(me == 0, jnp.zeros_like(low), low)
            high = jnp.where(me == count - 1, jnp.zeros_like(high), high)
        cells = jnp.concatenate([low, cells, high], axis=dim)
    return cells


def scatter_sum(blocks, axis, dim):
    count = lax.axis_size(axis)
    if count == 1:
        return lax.index_in_dim(blocks, 0, dim, keepdims=False)
    if count > 4:
        return lax.psum_scatter(blocks, axis, scatter_dimension=dim, tiled=False)
    me = lax.axis_index(axis)
    total = lax.dynamic_index_in_dim(blocks, me, dim, keepdims=False)
    for shift in range(1, count):
        part = lax.dynamic_index_in_dim(blocks, (me + shift) % count, dim, keepdims=False)
        total = total + lax.ppermute(part, axis, [(j, (j + shift) % count) for j in range(count)])
    return total


def take_rows(pieces, start, count):
    step = pieces[0].shape[0]
    out = []
    row = start
    while row < start + count:
        at = row % step
        take = min(start + count - row, step - at)
        out.append(pieces[row // step][at : at + take])
        row += take
    return jnp.concatenate(out, axis=0) if len(out) > 1 else out[0]


def on_device(x_act, grad_out, weight):
    size_x, size_y, depth, chans = x_act.shape
    ncores = lax.axis_size("col")
    half = weight.shape[2] // ncores
    offset = lax.axis_index("col") * half
    gh = with_halo(grad_out, (("gx", 0), ("gy", 1)), 1)
    taps = weight.reshape(3, 3, 3, chans, weight.shape[2])
    kflip = jnp.transpose(taps[::-1, ::-1, ::-1], (0, 1, 2, 4, 3))
    pad = [(0, 0), (0, 0), (1, 1)]
    inner = lax.conv_general_dilated(
        gh[None], kflip, (1, 1, 1), pad,
        dimension_numbers=("NDHWC", "DHWIO", "NDHWC"),
        preferred_element_type=jnp.float32,
    )[0]
    grad_in = inner.astype(jnp.bfloat16)
    gshare = lax.dynamic_slice_in_dim(gh, offset, half, 3)
    gdeep = jnp.pad(gshare, ((0, 0), (0, 0), (1, 1), (0, 0)))
    stack = jnp.concatenate([lax.slice_in_dim(gdeep, 2 - c, 2 - c + depth, axis=2) for c in range(3)], axis=3)
    pieces = []
    for a in range(3):
        for b in range(3):
            window = stack[2 - a : 2 - a + size_x, 2 - b : 2 - b + size_y]
            term = lax.dot_general(
                x_act, window, (((0, 1, 2), (0, 1, 2)), ((), ())), preferred_element_type=jnp.float32
            )
            pieces.append(jnp.transpose(term.reshape(chans, 3, half), (1, 0, 2)).reshape(3 * chans, half))
    nx = lax.axis_size("gx")
    ny = lax.axis_size("gy")
    owned_rows = 27 * chans // (nx * ny)
    if ny == 2:
        iy = lax.axis_index("gy")
        side = [
            jnp.stack([take_rows(pieces, (gx * 2 + y) * owned_rows, owned_rows) for gx in range(nx)])
            for y in range(2)
        ]
        split = owned_rows // 2 if owned_rows % 16 == 0 else owned_rows
        parts = []
        for lo, hi in ((0, split), (split, owned_rows)):
            if lo == hi:
                continue
            keep = jnp.where(iy == 0, side[0][:, lo:hi], side[1][:, lo:hi])
            send = jnp.where(iy == 0, side[1][:, lo:hi], side[0][:, lo:hi])
            partial = keep + lax.ppermute(send, "gy", [(0, 1), (1, 0)])
            parts.append(scatter_sum(partial, "gx", 0))
        owned = jnp.concatenate(parts, axis=0) if len(parts) > 1 else parts[0]
    else:
        weight_terms = jnp.concatenate(pieces, axis=0)
        blocks = weight_terms.reshape(nx, ny, owned_rows, half)
        owned = scatter_sum(scatter_sum(blocks, "gy", 1), "gx", 0)
    total_cells = size_x * lax.axis_size("gx") * size_y * lax.axis_size("gy") * depth
    grad_weight = owned / jnp.sqrt(jnp.float32(total_cells))
    return (grad_in, grad_weight)


def solution(mesh):
    return jax.shard_map(
        on_device,
        mesh=mesh,
        in_specs=(P(("grp", "gx"), "gy", None, None), P(("grp", "gx"), "gy", None, None), P()),
        out_specs=(P(("grp", "gx"), "gy", None, None), P(("grp", "gx", "gy"), "col")),
        check_vma=False,
    )
```

```python
import jax
import jax.numpy as jnp
from jax import lax
from jax.sharding import PartitionSpec as P


def with_halo(cells, sides, width):
    for axis, dim in sides:
        count = lax.axis_size(axis)
        head = lax.slice_in_dim(cells, 0, width, axis=dim)
        tail = lax.slice_in_dim(cells, cells.shape[dim] - width, cells.shape[dim], axis=dim)
        if count == 1:
            low = jnp.zeros_like(tail)
            high = jnp.zeros_like(head)
        elif count == 2:
            me = lax.axis_index(axis)
            got = lax.ppermute(jnp.where(me == 0, tail, head), axis, [(0, 1), (1, 0)])
            low = jnp.where(me == 1, got, jnp.zeros_like(got))
            high = jnp.where(me == 0, got, jnp.zeros_like(got))
        else:
            me = lax.axis_index(axis)
            low = lax.ppermute(tail, axis, [(i, (i + 1) % count) for i in range(count)])
            high = lax.ppermute(head, axis, [((i + 1) % count, i) for i in range(count)])
            low = jnp.where(me == 0, jnp.zeros_like(low), low)
            high = jnp.where(me == count - 1, jnp.zeros_like(high), high)
        cells = jnp.concatenate([low, cells, high], axis=dim)
    return cells


def scatter_sum(blocks, axis, dim):
    count = lax.axis_size(axis)
    if count == 1:
        return lax.index_in_dim(blocks, 0, dim, keepdims=False)
    if count > 4:
        return lax.psum_scatter(blocks, axis, scatter_dimension=dim, tiled=False)
    me = lax.axis_index(axis)
    total = lax.dynamic_index_in_dim(blocks, me, dim, keepdims=False)
    for shift in sorted(range(1, count), key=lambda s: -min(s, count - s)):
        part = lax.dynamic_index_in_dim(blocks, (me + shift) % count, dim, keepdims=False)
        total = total + lax.ppermute(part, axis, [(j, (j + shift) % count) for j in range(count)])
    return total


def take_rows(pieces, start, count):
    step = pieces[0].shape[0]
    out = []
    row = start
    while row < start + count:
        at = row % step
        take = min(start + count - row, step - at)
        out.append(pieces[row // step][at : at + take])
        row += take
    return jnp.concatenate(out, axis=0) if len(out) > 1 else out[0]


def on_device(x_act, grad_out, weight):
    size_x, size_y, depth, chans = x_act.shape
    ncores = lax.axis_size("col")
    half = weight.shape[2] // ncores
    offset = lax.axis_index("col") * half
    gh = with_halo(grad_out, (("gy", 1), ("gx", 0)), 1)
    taps = weight.reshape(3, 3, 3, chans, weight.shape[2])
    kflip = jnp.transpose(taps[::-1, ::-1, ::-1], (0, 1, 2, 4, 3))
    pad = [(0, 0), (0, 0), (1, 1)]
    inner = lax.conv_general_dilated(
        gh[None], kflip, (1, 1, 1), pad,
        dimension_numbers=("NDHWC", "DHWIO", "NDHWC"),
        preferred_element_type=jnp.float32,
    )[0]
    grad_in = inner.astype(jnp.bfloat16)
    gshare = lax.dynamic_slice_in_dim(gh, offset, half, 3)
    gdeep = jnp.pad(gshare, ((0, 0), (0, 0), (1, 1), (0, 0)))
    stack = jnp.concatenate([lax.slice_in_dim(gdeep, 2 - c, 2 - c + depth, axis=2) for c in range(3)], axis=3)
    pieces = []
    for a in range(3):
        for b in range(3):
            window = stack[2 - a : 2 - a + size_x, 2 - b : 2 - b + size_y]
            term = lax.dot_general(
                x_act, window, (((0, 1, 2), (0, 1, 2)), ((), ())), preferred_element_type=jnp.float32
            )
            pieces.append(jnp.transpose(term.reshape(chans, 3, half), (1, 0, 2)).reshape(3 * chans, half))
    nx = lax.axis_size("gx")
    ny = lax.axis_size("gy")
    owned_rows = 27 * chans // (nx * ny)
    if ny == 2:
        iy = lax.axis_index("gy")
        side = [
            jnp.stack([take_rows(pieces, (gx * 2 + y) * owned_rows, owned_rows) for gx in range(nx)])
            for y in range(2)
        ]
        split = owned_rows // 2 if owned_rows % 16 == 0 else owned_rows
        parts = []
        for lo, hi in ((0, split), (split, owned_rows)):
            if lo == hi:
                continue
            keep = jnp.where(iy == 0, side[0][:, lo:hi], side[1][:, lo:hi])
            send = jnp.where(iy == 0, side[1][:, lo:hi], side[0][:, lo:hi])
            partial = keep + lax.ppermute(send, "gy", [(0, 1), (1, 0)])
            parts.append(scatter_sum(partial, "gx", 0))
        owned = jnp.concatenate(parts, axis=0) if len(parts) > 1 else parts[0]
    else:
        weight_terms = jnp.concatenate(pieces, axis=0)
        blocks = weight_terms.reshape(nx, ny, owned_rows, half)
        owned = scatter_sum(scatter_sum(blocks, "gy", 1), "gx", 0)
    total_cells = size_x * lax.axis_size("gx") * size_y * lax.axis_size("gy") * depth
    grad_weight = owned / jnp.sqrt(jnp.float32(total_cells))
    return (grad_in, grad_weight)


def solution(mesh):
    return jax.shard_map(
        on_device,
        mesh=mesh,
        in_specs=(P(("grp", "gx"), "gy", None, None), P(("grp", "gx"), "gy", None, None), P()),
        out_specs=(P(("grp", "gx"), "gy", None, None), P(("grp", "gx", "gy"), "col")),
        check_vma=False,
    )
```

```python
import jax
import jax.numpy as jnp
from jax import lax
from jax.sharding import PartitionSpec as P


def halo_parts(cells, sides, width):
    got = []
    for axis, dim in sides:
        count = lax.axis_size(axis)
        head = lax.slice_in_dim(cells, 0, width, axis=dim)
        tail = lax.slice_in_dim(cells, cells.shape[dim] - width, cells.shape[dim], axis=dim)
        if count == 1:
            low = jnp.zeros_like(tail)
            high = jnp.zeros_like(head)
        elif count == 2:
            me = lax.axis_index(axis)
            recv = lax.ppermute(jnp.where(me == 0, tail, head), axis, [(0, 1), (1, 0)])
            low = jnp.where(me == 1, recv, jnp.zeros_like(recv))
            high = jnp.where(me == 0, recv, jnp.zeros_like(recv))
        else:
            me = lax.axis_index(axis)
            low = lax.ppermute(tail, axis, [(i, (i + 1) % count) for i in range(count)])
            high = lax.ppermute(head, axis, [((i + 1) % count, i) for i in range(count)])
            low = jnp.where(me == 0, jnp.zeros_like(low), low)
            high = jnp.where(me == count - 1, jnp.zeros_like(high), high)
        got.append((dim, low, high))
        cells = jnp.concatenate([low, cells, high], axis=dim)
    return got


def assemble(cells, got, lo, hi):
    cells = lax.slice_in_dim(cells, lo, hi, axis=3)
    for dim, low, high in got:
        cells = jnp.concatenate(
            [lax.slice_in_dim(low, lo, hi, axis=3), cells, lax.slice_in_dim(high, lo, hi, axis=3)], axis=dim
        )
    return cells


def scatter_sum(blocks, axis, dim):
    count = lax.axis_size(axis)
    if count == 1:
        return lax.index_in_dim(blocks, 0, dim, keepdims=False)
    if count > 4:
        return lax.psum_scatter(blocks, axis, scatter_dimension=dim, tiled=False)
    me = lax.axis_index(axis)
    total = lax.dynamic_index_in_dim(blocks, me, dim, keepdims=False)
    for shift in range(1, count):
        part = lax.dynamic_index_in_dim(blocks, (me + shift) % count, dim, keepdims=False)
        total = total + lax.ppermute(part, axis, [(j, (j + shift) % count) for j in range(count)])
    return total


def take_rows(pieces, start, count):
    step = pieces[0].shape[0]
    out = []
    row = start
    while row < start + count:
        at = row % step
        take = min(start + count - row, step - at)
        out.append(pieces[row // step][at : at + take])
        row += take
    return jnp.concatenate(out, axis=0) if len(out) > 1 else out[0]


def on_device(x_act, grad_out, weight):
    size_x, size_y, depth, chans = x_act.shape
    ncores = lax.axis_size("col")
    half = weight.shape[2] // ncores
    offset = lax.axis_index("col") * half
    got = halo_parts(grad_out, (("gy", 1), ("gx", 0)), 1)
    gh = assemble(grad_out, got, 0, chans)
    taps = weight.reshape(3, 3, 3, chans, weight.shape[2])
    kflip = jnp.transpose(taps[::-1, ::-1, ::-1], (0, 1, 2, 4, 3))
    pad = [(0, 0), (0, 0), (1, 1)]
    inner = lax.conv_general_dilated(
        gh[None], kflip, (1, 1, 1), pad,
        dimension_numbers=("NDHWC", "DHWIO", "NDHWC"),
        preferred_element_type=jnp.float32,
    )[0]
    grad_in = inner.astype(jnp.bfloat16)
    if ncores == 1:
        gshare = assemble(grad_out, got, 0, half)
    else:
        gshare = jnp.where(
            lax.axis_index("col") == 0, assemble(grad_out, got, 0, half), assemble(grad_out, got, half, 2 * half)
        )
    gdeep = jnp.pad(gshare, ((0, 0), (0, 0), (1, 1), (0, 0)))
    stack = jnp.concatenate([lax.slice_in_dim(gdeep, 2 - c, 2 - c + depth, axis=2) for c in range(3)], axis=3)
    pieces = []
    for a in range(3):
        for b in range(3):
            window = stack[2 - a : 2 - a + size_x, 2 - b : 2 - b + size_y]
            term = lax.dot_general(
                x_act, window, (((0, 1, 2), (0, 1, 2)), ((), ())), preferred_element_type=jnp.float32
            )
            pieces.append(jnp.transpose(term.reshape(chans, 3, half), (1, 0, 2)).reshape(3 * chans, half))
    nx = lax.axis_size("gx")
    ny = lax.axis_size("gy")
    owned_rows = 27 * chans // (nx * ny)
    if ny == 2:
        iy = lax.axis_index("gy")
        side = [
            jnp.stack([take_rows(pieces, (gx * 2 + y) * owned_rows, owned_rows) for gx in range(nx)])
            for y in range(2)
        ]
        split = owned_rows // 2 if owned_rows % 16 == 0 else owned_rows
        parts = []
        for lo, hi in ((0, split), (split, owned_rows)):
            if lo == hi:
                continue
            keep = jnp.where(iy == 0, side[0][:, lo:hi], side[1][:, lo:hi])
            send = jnp.where(iy == 0, side[1][:, lo:hi], side[0][:, lo:hi])
            partial = keep + lax.ppermute(send, "gy", [(0, 1), (1, 0)])
            parts.append(scatter_sum(partial, "gx", 0))
        owned = jnp.concatenate(parts, axis=0) if len(parts) > 1 else parts[0]
    else:
        weight_terms = jnp.concatenate(pieces, axis=0)
        blocks = weight_terms.reshape(nx, ny, owned_rows, half)
        owned = scatter_sum(scatter_sum(blocks, "gy", 1), "gx", 0)
    total_cells = size_x * lax.axis_size("gx") * size_y * lax.axis_size("gy") * depth
    grad_weight = owned / jnp.sqrt(jnp.float32(total_cells))
    return (grad_in, grad_weight)


def solution(mesh):
    return jax.shard_map(
        on_device,
        mesh=mesh,
        in_specs=(P(("grp", "gx"), "gy", None, None), P(("grp", "gx"), "gy", None, None), P()),
        out_specs=(P(("grp", "gx"), "gy", None, None), P(("grp", "gx", "gy"), "col")),
        check_vma=False,
    )
```

```python
import jax
import jax.numpy as jnp
from jax import lax
from jax.sharding import PartitionSpec as P


def halo_parts(cells, sides, width):
    got = []
    for axis, dim in sides:
        count = lax.axis_size(axis)
        head = lax.slice_in_dim(cells, 0, width, axis=dim)
        tail = lax.slice_in_dim(cells, cells.shape[dim] - width, cells.shape[dim], axis=dim)
        if count == 1:
            low = jnp.zeros_like(tail)
            high = jnp.zeros_like(head)
        elif count == 2:
            me = lax.axis_index(axis)
            edge = lax.dynamic_slice_in_dim(cells, (1 - me) * (cells.shape[dim] - width), width, axis=dim)
            recv = lax.ppermute(edge, axis, [(0, 1), (1, 0)])
            low = jnp.where(me == 1, recv, jnp.zeros_like(recv))
            high = jnp.where(me == 0, recv, jnp.zeros_like(recv))
        else:
            me = lax.axis_index(axis)
            low = lax.ppermute(tail, axis, [(i, (i + 1) % count) for i in range(count)])
            high = lax.ppermute(head, axis, [((i + 1) % count, i) for i in range(count)])
            low = jnp.where(me == 0, jnp.zeros_like(low), low)
            high = jnp.where(me == count - 1, jnp.zeros_like(high), high)
        got.append((dim, low, high))
        cells = jnp.concatenate([low, cells, high], axis=dim)
    return got


def assemble(cells, got, lo, hi):
    cells = lax.slice_in_dim(cells, lo, hi, axis=3)
    for dim, low, high in got:
        cells = jnp.concatenate(
            [lax.slice_in_dim(low, lo, hi, axis=3), cells, lax.slice_in_dim(high, lo, hi, axis=3)], axis=dim
        )
    return cells


def scatter_sum(blocks, axis, dim):
    count = lax.axis_size(axis)
    if count == 1:
        return lax.index_in_dim(blocks, 0, dim, keepdims=False)
    if count > 4:
        return lax.psum_scatter(blocks, axis, scatter_dimension=dim, tiled=False)
    me = lax.axis_index(axis)
    total = lax.dynamic_index_in_dim(blocks, me, dim, keepdims=False)
    for shift in range(1, count):
        part = lax.dynamic_index_in_dim(blocks, (me + shift) % count, dim, keepdims=False)
        total = total + lax.ppermute(part, axis, [(j, (j + shift) % count) for j in range(count)])
    return total


def take_rows(pieces, start, count):
    step = pieces[0].shape[0]
    out = []
    row = start
    while row < start + count:
        at = row % step
        take = min(start + count - row, step - at)
        out.append(pieces[row // step][at : at + take])
        row += take
    return jnp.concatenate(out, axis=0) if len(out) > 1 else out[0]


def on_device(x_act, grad_out, weight):
    size_x, size_y, depth, chans = x_act.shape
    ncores = lax.axis_size("col")
    half = weight.shape[2] // ncores
    offset = lax.axis_index("col") * half
    got = halo_parts(grad_out, (("gy", 1), ("gx", 0)), 1)
    gh = assemble(grad_out, got, 0, chans)
    taps = weight.reshape(3, 3, 3, chans, weight.shape[2])
    kflip = jnp.transpose(taps[::-1, ::-1, ::-1], (0, 1, 2, 4, 3))
    pad = [(0, 0), (0, 0), (1, 1)]
    inner = lax.conv_general_dilated(
        gh[None], kflip, (1, 1, 1), pad,
        dimension_numbers=("NDHWC", "DHWIO", "NDHWC"),
        preferred_element_type=jnp.float32,
    )[0]
    grad_in = inner.astype(jnp.bfloat16)
    if ncores == 1:
        gshare = assemble(grad_out, got, 0, half)
    else:
        gshare = jnp.where(
            lax.axis_index("col") == 0, assemble(grad_out, got, 0, half), assemble(grad_out, got, half, 2 * half)
        )
    gdeep = jnp.pad(gshare, ((0, 0), (0, 0), (1, 1), (0, 0)))
    stack = jnp.concatenate([lax.slice_in_dim(gdeep, 2 - c, 2 - c + depth, axis=2) for c in range(3)], axis=3)
    pieces = []
    for a in range(3):
        for b in range(3):
            window = stack[2 - a : 2 - a + size_x, 2 - b : 2 - b + size_y]
            term = lax.dot_general(
                x_act, window, (((0, 1, 2), (0, 1, 2)), ((), ())), preferred_element_type=jnp.float32
            )
            pieces.append(jnp.transpose(term.reshape(chans, 3, half), (1, 0, 2)).reshape(3 * chans, half))
    nx = lax.axis_size("gx")
    ny = lax.axis_size("gy")
    owned_rows = 27 * chans // (nx * ny)
    if ny == 2:
        iy = lax.axis_index("gy")
        side = [
            jnp.stack([take_rows(pieces, (gx * 2 + y) * owned_rows, owned_rows) for gx in range(nx)])
            for y in range(2)
        ]
        split = owned_rows // 2 if owned_rows % 16 == 0 else owned_rows
        parts = []
        for lo, hi in ((0, split), (split, owned_rows)):
            if lo == hi:
                continue
            keep = jnp.where(iy == 0, side[0][:, lo:hi], side[1][:, lo:hi])
            send = jnp.where(iy == 0, side[1][:, lo:hi], side[0][:, lo:hi])
            partial = keep + lax.ppermute(send, "gy", [(0, 1), (1, 0)])
            parts.append(scatter_sum(partial, "gx", 0))
        owned = jnp.concatenate(parts, axis=0) if len(parts) > 1 else parts[0]
    else:
        weight_terms = jnp.concatenate(pieces, axis=0)
        blocks = weight_terms.reshape(nx, ny, owned_rows, half)
        owned = scatter_sum(scatter_sum(blocks, "gy", 1), "gx", 0)
    total_cells = size_x * lax.axis_size("gx") * size_y * lax.axis_size("gy") * depth
    grad_weight = owned / jnp.sqrt(jnp.float32(total_cells))
    return (grad_in, grad_weight)


def solution(mesh):
    return jax.shard_map(
        on_device,
        mesh=mesh,
        in_specs=(P(("grp", "gx"), "gy", None, None), P(("grp", "gx"), "gy", None, None), P()),
        out_specs=(P(("grp", "gx"), "gy", None, None), P(("grp", "gx", "gy"), "col")),
        check_vma=False,
    )
```

```python
import jax
import jax.numpy as jnp
from jax import lax
from jax.sharding import PartitionSpec as P


def halo_parts(cells, sides, width):
    got = []
    for axis, dim in sides:
        count = lax.axis_size(axis)
        head = lax.slice_in_dim(cells, 0, width, axis=dim)
        tail = lax.slice_in_dim(cells, cells.shape[dim] - width, cells.shape[dim], axis=dim)
        if count == 1:
            low = jnp.zeros_like(tail)
            high = jnp.zeros_like(head)
        elif count == 2:
            me = lax.axis_index(axis)
            recv = lax.ppermute(jnp.where(me == 0, tail, head), axis, [(0, 1), (1, 0)])
            low = jnp.where(me == 1, recv, jnp.zeros_like(recv))
            high = jnp.where(me == 0, recv, jnp.zeros_like(recv))
        else:
            me = lax.axis_index(axis)
            low = lax.ppermute(tail, axis, [(i, (i + 1) % count) for i in range(count)])
            high = lax.ppermute(head, axis, [((i + 1) % count, i) for i in range(count)])
            low = jnp.where(me == 0, jnp.zeros_like(low), low)
            high = jnp.where(me == count - 1, jnp.zeros_like(high), high)
        got.append((dim, low, high))
        cells = jnp.concatenate([low, cells, high], axis=dim)
    return got


def assemble(cells, got, lo, hi):
    cells = lax.slice_in_dim(cells, lo, hi, axis=3)
    for dim, low, high in got:
        cells = jnp.concatenate(
            [lax.slice_in_dim(low, lo, hi, axis=3), cells, lax.slice_in_dim(high, lo, hi, axis=3)], axis=dim
        )
    return cells


def scatter_sum(blocks, axis, dim):
    count = lax.axis_size(axis)
    if count == 1:
        return lax.index_in_dim(blocks, 0, dim, keepdims=False)
    if count > 4:
        return lax.psum_scatter(blocks, axis, scatter_dimension=dim, tiled=False)
    me = lax.axis_index(axis)
    total = lax.dynamic_index_in_dim(blocks, me, dim, keepdims=False)
    for shift in range(1, count):
        part = lax.dynamic_index_in_dim(blocks, (me + shift) % count, dim, keepdims=False)
        total = total + lax.ppermute(part, axis, [(j, (j + shift) % count) for j in range(count)])
    return total


def take_rows(pieces, start, count):
    step = pieces[0].shape[0]
    out = []
    row = start
    while row < start + count:
        at = row % step
        take = min(start + count - row, step - at)
        out.append(pieces[row // step][at : at + take])
        row += take
    return jnp.concatenate(out, axis=0) if len(out) > 1 else out[0]


def on_device(x_act, grad_out, weight):
    size_x, size_y, depth, chans = x_act.shape
    ncores = lax.axis_size("col")
    half = weight.shape[2] // ncores
    offset = lax.axis_index("col") * half
    got = halo_parts(grad_out, (("gy", 1), ("gx", 0)), 1)
    gh = assemble(grad_out, got, 0, chans)
    taps = weight.reshape(3, 3, 3, chans, weight.shape[2])
    kflip = jnp.transpose(taps[::-1, ::-1, ::-1], (0, 1, 2, 4, 3))
    pad = [(0, 0), (0, 0), (1, 1)]
    inner = lax.conv_general_dilated(
        gh[None], kflip, (1, 1, 1), pad,
        dimension_numbers=("NDHWC", "DHWIO", "NDHWC"),
        preferred_element_type=jnp.float32,
    )[0]
    grad_in = inner.astype(jnp.bfloat16)
    if ncores == 1:
        gshare = assemble(grad_out, got, 0, half)
    else:
        gshare = jnp.where(
            lax.axis_index("col") == 0, assemble(grad_out, got, 0, half), assemble(grad_out, got, half, 2 * half)
        )
    gdeep = jnp.pad(gshare, ((0, 0), (0, 0), (1, 1), (0, 0)))
    stack = jnp.concatenate([lax.slice_in_dim(gdeep, 2 - c, 2 - c + depth, axis=2) for c in range(3)], axis=3)
    pieces = []
    for a in range(3):
        for b in range(3):
            window = stack[2 - a : 2 - a + size_x, 2 - b : 2 - b + size_y]
            term = lax.dot_general(
                x_act, window, (((0, 1, 2), (0, 1, 2)), ((), ())), preferred_element_type=jnp.float32
            )
            pieces.append(jnp.transpose(term.reshape(chans, 3, half), (1, 0, 2)).reshape(3 * chans, half))
    nx = lax.axis_size("gx")
    ny = lax.axis_size("gy")
    owned_rows = 27 * chans // (nx * ny)
    if ny == 2:
        iy = lax.axis_index("gy")
        side = [
            jnp.stack([take_rows(pieces, (gx * 2 + y) * owned_rows, owned_rows) for gx in range(nx)])
            for y in range(2)
        ]
        split = owned_rows // 2 if owned_rows % 16 == 0 else owned_rows
        parts = []
        for lo, hi in ((0, split), (split, owned_rows)):
            if lo == hi:
                continue
            keep = jnp.where(iy == 0, side[0][:, lo:hi], side[1][:, lo:hi])
            send = jnp.where(iy == 0, side[1][:, lo:hi], side[0][:, lo:hi])
            partial = keep + lax.ppermute(send, "gy", [(0, 1), (1, 0)])
            last = partial
            parts.append(scatter_sum(partial, "gx", 0))
        grad_in = lax.optimization_barrier((grad_in, last))[0]
        owned = jnp.concatenate(parts, axis=0) if len(parts) > 1 else parts[0]
    else:
        weight_terms = jnp.concatenate(pieces, axis=0)
        blocks = weight_terms.reshape(nx, ny, owned_rows, half)
        owned = scatter_sum(scatter_sum(blocks, "gy", 1), "gx", 0)
    total_cells = size_x * lax.axis_size("gx") * size_y * lax.axis_size("gy") * depth
    grad_weight = owned / jnp.sqrt(jnp.float32(total_cells))
    return (grad_in, grad_weight)


def solution(mesh):
    return jax.shard_map(
        on_device,
        mesh=mesh,
        in_specs=(P(("grp", "gx"), "gy", None, None), P(("grp", "gx"), "gy", None, None), P()),
        out_specs=(P(("grp", "gx"), "gy", None, None), P(("grp", "gx", "gy"), "col")),
        check_vma=False,
    )
```

```python
import jax
import jax.numpy as jnp
from jax import lax
from jax.sharding import PartitionSpec as P


def halo_parts(cells, sides, width):
    got = []
    for axis, dim in sides:
        count = lax.axis_size(axis)
        head = lax.slice_in_dim(cells, 0, width, axis=dim)
        tail = lax.slice_in_dim(cells, cells.shape[dim] - width, cells.shape[dim], axis=dim)
        if count == 1:
            low = jnp.zeros_like(tail)
            high = jnp.zeros_like(head)
        elif count == 2:
            me = lax.axis_index(axis)
            recv = lax.ppermute(jnp.where(me == 0, tail, head), axis, [(0, 1), (1, 0)])
            low = jnp.where(me == 1, recv, jnp.zeros_like(recv))
            high = jnp.where(me == 0, recv, jnp.zeros_like(recv))
        else:
            me = lax.axis_index(axis)
            low = lax.ppermute(tail, axis, [(i, (i + 1) % count) for i in range(count)])
            high = lax.ppermute(head, axis, [((i + 1) % count, i) for i in range(count)])
            low = jnp.where(me == 0, jnp.zeros_like(low), low)
            high = jnp.where(me == count - 1, jnp.zeros_like(high), high)
        got.append((dim, low, high))
        cells = jnp.concatenate([low, cells, high], axis=dim)
    return got


def assemble(cells, got, lo, hi):
    cells = lax.slice_in_dim(cells, lo, hi, axis=3)
    for dim, low, high in got:
        cells = jnp.concatenate(
            [lax.slice_in_dim(low, lo, hi, axis=3), cells, lax.slice_in_dim(high, lo, hi, axis=3)], axis=dim
        )
    return cells


def scatter_sum(blocks, axis, dim):
    count = lax.axis_size(axis)
    if count == 1:
        return lax.index_in_dim(blocks, 0, dim, keepdims=False)
    if count > 4:
        return lax.psum_scatter(blocks, axis, scatter_dimension=dim, tiled=False)
    me = lax.axis_index(axis)
    total = lax.dynamic_index_in_dim(blocks, me, dim, keepdims=False)
    for shift in range(1, count):
        part = lax.dynamic_index_in_dim(blocks, (me + shift) % count, dim, keepdims=False)
        total = total + lax.ppermute(part, axis, [(j, (j + shift) % count) for j in range(count)])
    return total


def take_rows(pieces, start, count):
    step = pieces[0].shape[0]
    out = []
    row = start
    while row < start + count:
        at = row % step
        take = min(start + count - row, step - at)
        out.append(pieces[row // step][at : at + take])
        row += take
    return jnp.concatenate(out, axis=0) if len(out) > 1 else out[0]


def on_device(x_act, grad_out, weight):
    size_x, size_y, depth, chans = x_act.shape
    ncores = lax.axis_size("col")
    half = weight.shape[2] // ncores
    offset = lax.axis_index("col") * half
    got = halo_parts(grad_out, (("gy", 1), ("gx", 0)), 1)
    gh = assemble(grad_out, got, 0, chans)
    taps = weight.reshape(3, 3, 3, chans, weight.shape[2])
    kflip = jnp.transpose(taps[::-1, ::-1, ::-1], (0, 1, 2, 4, 3))
    pad = [(0, 0), (0, 0), (1, 1)]
    inner = lax.conv_general_dilated(
        gh[None], kflip, (1, 1, 1), pad,
        dimension_numbers=("NDHWC", "DHWIO", "NDHWC"),
        preferred_element_type=jnp.float32,
    )[0]
    grad_in = inner.astype(jnp.bfloat16)
    def share_stack(piece):
        if ncores == 1:
            mine = piece[..., :half]
        else:
            mine = lax.dynamic_slice_in_dim(piece, offset, half, 3)
        deep = jnp.pad(mine, ((0, 0), (0, 0), (1, 1), (0, 0)))
        return jnp.concatenate([lax.slice_in_dim(deep, 2 - c, 2 - c + depth, axis=2) for c in range(3)], axis=3)

    stack = share_stack(grad_out)
    for dim, low, high in got:
        stack = jnp.concatenate([share_stack(low), stack, share_stack(high)], axis=dim)
    pieces = []
    for a in range(3):
        for b in range(3):
            window = stack[2 - a : 2 - a + size_x, 2 - b : 2 - b + size_y]
            term = lax.dot_general(
                x_act, window, (((0, 1, 2), (0, 1, 2)), ((), ())), preferred_element_type=jnp.float32
            )
            pieces.append(jnp.transpose(term.reshape(chans, 3, half), (1, 0, 2)).reshape(3 * chans, half))
    nx = lax.axis_size("gx")
    ny = lax.axis_size("gy")
    owned_rows = 27 * chans // (nx * ny)
    if ny == 2:
        iy = lax.axis_index("gy")
        side = [
            jnp.stack([take_rows(pieces, (gx * 2 + y) * owned_rows, owned_rows) for gx in range(nx)])
            for y in range(2)
        ]
        split = owned_rows // 2 if owned_rows % 16 == 0 else owned_rows
        parts = []
        for lo, hi in ((0, split), (split, owned_rows)):
            if lo == hi:
                continue
            keep = jnp.where(iy == 0, side[0][:, lo:hi], side[1][:, lo:hi])
            send = jnp.where(iy == 0, side[1][:, lo:hi], side[0][:, lo:hi])
            partial = keep + lax.ppermute(send, "gy", [(0, 1), (1, 0)])
            parts.append(scatter_sum(partial, "gx", 0))
        owned = jnp.concatenate(parts, axis=0) if len(parts) > 1 else parts[0]
    else:
        weight_terms = jnp.concatenate(pieces, axis=0)
        blocks = weight_terms.reshape(nx, ny, owned_rows, half)
        owned = scatter_sum(scatter_sum(blocks, "gy", 1), "gx", 0)
    total_cells = size_x * lax.axis_size("gx") * size_y * lax.axis_size("gy") * depth
    grad_weight = owned / jnp.sqrt(jnp.float32(total_cells))
    return (grad_in, grad_weight)


def solution(mesh):
    return jax.shard_map(
        on_device,
        mesh=mesh,
        in_specs=(P(("grp", "gx"), "gy", None, None), P(("grp", "gx"), "gy", None, None), P()),
        out_specs=(P(("grp", "gx"), "gy", None, None), P(("grp", "gx", "gy"), "col")),
        check_vma=False,
    )
```

```python
import jax
import jax.numpy as jnp
from jax import lax
from jax.sharding import PartitionSpec as P


def halo_parts(cells, sides, width):
    got = []
    for axis, dim in sides:
        count = lax.axis_size(axis)
        head = lax.slice_in_dim(cells, 0, width, axis=dim)
        tail = lax.slice_in_dim(cells, cells.shape[dim] - width, cells.shape[dim], axis=dim)
        if count == 1:
            low = jnp.zeros_like(tail)
            high = jnp.zeros_like(head)
        elif count == 2:
            me = lax.axis_index(axis)
            recv = lax.ppermute(jnp.where(me == 0, tail, head), axis, [(0, 1), (1, 0)])
            low = jnp.where(me == 1, recv, jnp.zeros_like(recv))
            high = jnp.where(me == 0, recv, jnp.zeros_like(recv))
        else:
            me = lax.axis_index(axis)
            low = lax.ppermute(tail, axis, [(i, (i + 1) % count) for i in range(count)])
            high = lax.ppermute(head, axis, [((i + 1) % count, i) for i in range(count)])
            low = jnp.where(me == 0, jnp.zeros_like(low), low)
            high = jnp.where(me == count - 1, jnp.zeros_like(high), high)
        got.append((dim, low, high))
        cells = jnp.concatenate([low, cells, high], axis=dim)
    return got


def assemble(cells, got, lo, hi):
    cells = lax.slice_in_dim(cells, lo, hi, axis=3)
    for dim, low, high in got:
        cells = jnp.concatenate(
            [lax.slice_in_dim(low, lo, hi, axis=3), cells, lax.slice_in_dim(high, lo, hi, axis=3)], axis=dim
        )
    return cells


def scatter_sum(blocks, axis, dim):
    count = lax.axis_size(axis)
    if count == 1:
        return lax.index_in_dim(blocks, 0, dim, keepdims=False)
    if count > 4:
        return lax.psum_scatter(blocks, axis, scatter_dimension=dim, tiled=False)
    me = lax.axis_index(axis)
    total = lax.dynamic_index_in_dim(blocks, me, dim, keepdims=False)
    for shift in range(1, count):
        part = lax.dynamic_index_in_dim(blocks, (me + shift) % count, dim, keepdims=False)
        total = total + lax.ppermute(part, axis, [(j, (j + shift) % count) for j in range(count)])
    return total


def take_rows(pieces, start, count):
    step = pieces[0].shape[0]
    out = []
    row = start
    while row < start + count:
        at = row % step
        take = min(start + count - row, step - at)
        out.append(pieces[row // step][at : at + take])
        row += take
    return jnp.concatenate(out, axis=0) if len(out) > 1 else out[0]


def on_device(x_act, grad_out, weight):
    size_x, size_y, depth, chans = x_act.shape
    ncores = lax.axis_size("col")
    half = weight.shape[2] // ncores
    offset = lax.axis_index("col") * half
    got = halo_parts(grad_out, (("gy", 1), ("gx", 0)), 1)
    gh = assemble(grad_out, got, 0, chans)
    taps = weight.reshape(3, 3, 3, chans, weight.shape[2])
    kflip = jnp.transpose(taps[::-1, ::-1, ::-1], (0, 1, 2, 4, 3))
    pad = [(0, 0), (0, 0), (1, 1)]
    inner = lax.conv_general_dilated(
        gh[None], kflip, (1, 1, 1), pad,
        dimension_numbers=("NDHWC", "DHWIO", "NDHWC"),
        preferred_element_type=jnp.float32,
    )[0]
    grad_in = inner.astype(jnp.bfloat16)
    if ncores == 1:
        gshare = assemble(grad_out, got, 0, half)
    else:
        gshare = jnp.where(
            lax.axis_index("col") == 0, assemble(grad_out, got, 0, half), assemble(grad_out, got, half, 2 * half)
        )
    gdeep = jnp.pad(gshare, ((0, 0), (0, 0), (1, 1), (0, 0)))
    stack = jnp.concatenate([lax.slice_in_dim(gdeep, 2 - c, 2 - c + depth, axis=2) for c in range(3)], axis=3)
    pieces = []
    for a in range(3):
        for b in range(3):
            window = stack[2 - a : 2 - a + size_x, 2 - b : 2 - b + size_y]
            term = lax.dot_general(
                x_act, window, (((0, 1, 2), (0, 1, 2)), ((), ())), preferred_element_type=jnp.float32
            )
            pieces.append(jnp.transpose(term.reshape(chans, 3, half), (1, 0, 2)).reshape(3 * chans, half))
    nx = lax.axis_size("gx")
    ny = lax.axis_size("gy")
    owned_rows = 27 * chans // (nx * ny)
    if ny == 2:
        iy = lax.axis_index("gy")
        side = [
            jnp.stack([take_rows(pieces, (gx * 2 + y) * owned_rows, owned_rows) for gx in range(nx)])
            for y in range(2)
        ]
        cuts = 3 if owned_rows % 24 == 0 else 1
        bounds = [owned_rows * k // cuts for k in range(cuts + 1)]
        parts = []
        for lo, hi in zip(bounds[:-1], bounds[1:]):
            if lo == hi:
                continue
            keep = jnp.where(iy == 0, side[0][:, lo:hi], side[1][:, lo:hi])
            send = jnp.where(iy == 0, side[1][:, lo:hi], side[0][:, lo:hi])
            partial = keep + lax.ppermute(send, "gy", [(0, 1), (1, 0)])
            parts.append(scatter_sum(partial, "gx", 0))
        owned = jnp.concatenate(parts, axis=0) if len(parts) > 1 else parts[0]
    else:
        weight_terms = jnp.concatenate(pieces, axis=0)
        blocks = weight_terms.reshape(nx, ny, owned_rows, half)
        owned = scatter_sum(scatter_sum(blocks, "gy", 1), "gx", 0)
    total_cells = size_x * lax.axis_size("gx") * size_y * lax.axis_size("gy") * depth
    grad_weight = owned / jnp.sqrt(jnp.float32(total_cells))
    return (grad_in, grad_weight)


def solution(mesh):
    return jax.shard_map(
        on_device,
        mesh=mesh,
        in_specs=(P(("grp", "gx"), "gy", None, None), P(("grp", "gx"), "gy", None, None), P()),
        out_specs=(P(("grp", "gx"), "gy", None, None), P(("grp", "gx", "gy"), "col")),
        check_vma=False,
    )
```

```python
import jax
import jax.numpy as jnp
from jax import lax
from jax.sharding import PartitionSpec as P


def halo_parts(cells, sides, width):
    got = []
    for axis, dim in sides:
        count = lax.axis_size(axis)
        head = lax.slice_in_dim(cells, 0, width, axis=dim)
        tail = lax.slice_in_dim(cells, cells.shape[dim] - width, cells.shape[dim], axis=dim)
        if count == 1:
            low = jnp.zeros_like(tail)
            high = jnp.zeros_like(head)
        elif count == 2:
            me = lax.axis_index(axis)
            recv = lax.ppermute(jnp.where(me == 0, tail, head), axis, [(0, 1), (1, 0)])
            low = jnp.where(me == 1, recv, jnp.zeros_like(recv))
            high = jnp.where(me == 0, recv, jnp.zeros_like(recv))
        else:
            me = lax.axis_index(axis)
            low = lax.ppermute(tail, axis, [(i, (i + 1) % count) for i in range(count)])
            high = lax.ppermute(head, axis, [((i + 1) % count, i) for i in range(count)])
            low = jnp.where(me == 0, jnp.zeros_like(low), low)
            high = jnp.where(me == count - 1, jnp.zeros_like(high), high)
        got.append((dim, low, high))
        cells = jnp.concatenate([low, cells, high], axis=dim)
    return got


def assemble(cells, got, lo, hi):
    cells = lax.slice_in_dim(cells, lo, hi, axis=3)
    for dim, low, high in got:
        cells = jnp.concatenate(
            [lax.slice_in_dim(low, lo, hi, axis=3), cells, lax.slice_in_dim(high, lo, hi, axis=3)], axis=dim
        )
    return cells


def scatter_sum(blocks, axis, dim):
    count = lax.axis_size(axis)
    if count == 1:
        return lax.index_in_dim(blocks, 0, dim, keepdims=False)
    if count > 4:
        return lax.psum_scatter(blocks, axis, scatter_dimension=dim, tiled=False)
    me = lax.axis_index(axis)
    total = lax.dynamic_index_in_dim(blocks, me, dim, keepdims=False)
    for shift in sorted(range(1, count), key=lambda s: -min(s, count - s)):
        part = lax.dynamic_index_in_dim(blocks, (me + shift) % count, dim, keepdims=False)
        total = total + lax.ppermute(part, axis, [(j, (j + shift) % count) for j in range(count)])
    return total


def take_rows(pieces, start, count):
    step = pieces[0].shape[0]
    out = []
    row = start
    while row < start + count:
        at = row % step
        take = min(start + count - row, step - at)
        out.append(pieces[row // step][at : at + take])
        row += take
    return jnp.concatenate(out, axis=0) if len(out) > 1 else out[0]


def on_device(x_act, grad_out, weight):
    size_x, size_y, depth, chans = x_act.shape
    ncores = lax.axis_size("col")
    half = weight.shape[2] // ncores
    offset = lax.axis_index("col") * half
    got = halo_parts(grad_out, (("gy", 1), ("gx", 0)), 1)
    gh = assemble(grad_out, got, 0, chans)
    taps = weight.reshape(3, 3, 3, chans, weight.shape[2])
    kflip = jnp.transpose(taps[::-1, ::-1, ::-1], (0, 1, 2, 4, 3))
    pad = [(0, 0), (0, 0), (1, 1)]
    inner = lax.conv_general_dilated(
        gh[None], kflip, (1, 1, 1), pad,
        dimension_numbers=("NDHWC", "DHWIO", "NDHWC"),
        preferred_element_type=jnp.float32,
    )[0]
    grad_in = inner.astype(jnp.bfloat16)
    if ncores == 1:
        gshare = assemble(grad_out, got, 0, half)
    else:
        gshare = jnp.where(
            lax.axis_index("col") == 0, assemble(grad_out, got, 0, half), assemble(grad_out, got, half, 2 * half)
        )
    gdeep = jnp.pad(gshare, ((0, 0), (0, 0), (1, 1), (0, 0)))
    stack = jnp.concatenate([lax.slice_in_dim(gdeep, 2 - c, 2 - c + depth, axis=2) for c in range(3)], axis=3)
    pieces = []
    for a in range(3):
        for b in range(3):
            window = stack[2 - a : 2 - a + size_x, 2 - b : 2 - b + size_y]
            term = lax.dot_general(
                x_act, window, (((0, 1, 2), (0, 1, 2)), ((), ())), preferred_element_type=jnp.float32
            )
            pieces.append(jnp.transpose(term.reshape(chans, 3, half), (1, 0, 2)).reshape(3 * chans, half))
    nx = lax.axis_size("gx")
    ny = lax.axis_size("gy")
    owned_rows = 27 * chans // (nx * ny)
    if ny == 2:
        iy = lax.axis_index("gy")
        side = [
            jnp.stack([take_rows(pieces, (gx * 2 + y) * owned_rows, owned_rows) for gx in range(nx)])
            for y in range(2)
        ]
        split = owned_rows // 2 if owned_rows % 16 == 0 else owned_rows
        parts = []
        for lo, hi in ((0, split), (split, owned_rows)):
            if lo == hi:
                continue
            keep = jnp.where(iy == 0, side[0][:, lo:hi], side[1][:, lo:hi])
            send = jnp.where(iy == 0, side[1][:, lo:hi], side[0][:, lo:hi])
            partial = keep + lax.ppermute(send, "gy", [(0, 1), (1, 0)])
            parts.append(scatter_sum(partial, "gx", 0))
        owned = jnp.concatenate(parts, axis=0) if len(parts) > 1 else parts[0]
    else:
        weight_terms = jnp.concatenate(pieces, axis=0)
        blocks = weight_terms.reshape(nx, ny, owned_rows, half)
        owned = scatter_sum(scatter_sum(blocks, "gy", 1), "gx", 0)
    total_cells = size_x * lax.axis_size("gx") * size_y * lax.axis_size("gy") * depth
    grad_weight = owned / jnp.sqrt(jnp.float32(total_cells))
    return (grad_in, grad_weight)


def solution(mesh):
    return jax.shard_map(
        on_device,
        mesh=mesh,
        in_specs=(P(("grp", "gx"), "gy", None, None), P(("grp", "gx"), "gy", None, None), P()),
        out_specs=(P(("grp", "gx"), "gy", None, None), P(("grp", "gx", "gy"), "col")),
        check_vma=False,
    )
```
